128 devices in a mesh: scan: 16 (over y, x), tile: 8 (over z, core).
Axes of the slice: x: 4, y: 4, z: 4, core: 2. Of those that a mesh axis runs over, the one named last changes fastest.
Arguments:
- pointing: bfloat16 [16, 4096, 2048], P('tile', 'scan'), may hold values from -0.125 to 0.125
- ground_bin: int32 [16, 4096], P('tile', 'scan'), may hold values from 0 to 23
- degrees: int32 [16], P('tile'), may hold values from 2 to 8
- lengths: int32 [16], P('tile'), may hold values from 1 to 4096, 40960 in all
- tile_lists: int32 [16, 16], P('tile'), may hold values from 0 to 127, as said below
- owner_map: int32 [128], replicated, may hold values from 0 to 7, as said below
Outputs:
- obs_matrix: float32 [16384, 16384], P('tile', 'scan')
The draws below stay inside these ranges and needn't reach their ends.
Inputs may be any that keep to these rules, and one draw needn't show every extreme that they name: `owner_map`: for each j < 16, entries j * 8 to (j + 1) * 8 - 1 hold every owner 0 to 7 once. `tile_lists`: in each row, entries j * 1 to (j + 1) - 1 are distinct tiles of j * 8 to (j + 1) * 8 - 1; over the 2 rows of one index of tile, every owner is named (through owner_map) by exactly 4 entries.
All inputs are finite; a program needn't handle non-finite values. No bound on the sum of `lengths` on one device may be relied on, other than what follows from the above.
Results may differ from the reference program's by a relative error of at most 0.0003.
Values may be sent and summed in bfloat16 or wider, within the bound.
No kernel may reach another device: no remote copies, remote signals or barrier semaphores. Data moves between devices by JAX's collectives and lax.ppermute only.
A program may use at most 128 MiB of HBM per device.

```python
import math
import jax
import jax.numpy as jnp
import numpy as np
from jax import lax

TILE_PIX = 128
K = 16
SCAN_DEV = 2
DEG_MAX = 8
NGB = 24
NTPL = 32
NS = 4096
SCANS = 16
NTILE = 128
K_COL = 1
KP = 2048
N_SCAN = 16
N_TILE = 8


def owner_tables(key):
    base_key = jax.random.fold_in(key, 7)
    range_keys = jax.random.split(base_key, N_SCAN)
    return jax.vmap(lambda one_key: jax.random.permutation(one_key, N_TILE))(range_keys).astype(jnp.int32)


def draw_owner_map(key, part):
    return owner_tables(key).reshape(-1).astype(jnp.int32)


def draw_tile_lists(key, part):
    tables = owner_tables(key)
    inverse = jnp.argsort(tables, axis=1).astype(jnp.int32)
    device_keys = jax.random.split(jax.random.fold_in(key, 13), N_TILE)
    shuffles = jax.vmap(lambda one_key: jax.random.permutation(one_key, N_TILE))(device_keys).astype(jnp.int32)
    slots = jnp.arange(SCAN_DEV)[:, None] * K + jnp.arange(K)[None, :]
    owners = shuffles[:, slots % N_TILE]
    range_index = jnp.arange(K) // K_COL
    within = inverse[range_index[None, None, :], owners]
    tiles = range_index[None, None, :] * N_TILE + within
    return tiles.reshape(SCANS, K).astype(jnp.int32)


def with_ends(result, rng, least, top_value):
    extent = result.shape
    place = [jax.random.randint(jax.random.fold_in(rng, axis), (), 0, extent[axis]) for axis in range(len(extent))]
    result = result.at[tuple(place)].set(least)
    longest = extent.index(max(extent))
    place[longest] = (place[longest] + 1) % extent[longest]
    return result.at[tuple(place)].set(top_value)


def block_levels(stream_key, dims, shards, smallest, largest):
    def one(axis_at, blocks):
        draws = jax.random.uniform(jax.random.fold_in(jax.random.fold_in(stream_key, 6), axis_at), (blocks,), jnp.float32, smallest / len(shards), largest / len(shards))
        return jnp.repeat(jnp.exp(draws), dims[axis_at] // blocks).reshape((-1,) + (1,) * (len(dims) - axis_at - 1))

    factor_of = one(*shards[0])
    for cut in shards[1:]:
        factor_of = factor_of * one(*cut)
    return factor_of


def profile(count, total, most, skew):
    loads = [(1 << 20) // math.isqrt(grade ** skew) + 1 for grade in range(2, count + 1)]
    rest, holding = total - most - (count - 1), [1] * (count - 1)
    while rest > 0:
        movable = [i for i in range(count - 1) if holding[i] < most]
        mass, remaining = sum([loads[i] for i in movable]), rest
        for i in movable:
            addition = min(most - holding[i], max(1, remaining * loads[i] // mass), rest)
            holding[i] = holding[i] + addition
            rest = rest - addition
    return np.array([most] + holding)


def uneven_parts(rng, number_of, total, most, slope):
    if number_of == 2:
        one = jax.random.randint(rng, (), max(1, total - most), min(most, total - 1) + 1)
        return jnp.stack([one, total - one])
    sizes = jnp.asarray(profile(number_of, total, most, slope), jnp.int32)
    pairs = (number_of - 1) // 2
    donor, taker = sizes[1:1 + 2 * pairs:2], sizes[2:2 + 2 * pairs:2]
    room = jnp.minimum(donor - 1, most - taker)
    moved = jax.random.randint(jax.random.fold_in(rng, 1), (pairs,), 0, 1 << 20) % (room + 1)
    sizes = sizes.at[1:1 + 2 * pairs:2].set(donor - moved).at[2:2 + 2 * pairs:2].set(taker + moved)
    return sizes[jax.random.permutation(jax.random.fold_in(rng, 2), number_of)]


def noise(stream_key, dims, width, limit, shards=(), held_as=jnp.bfloat16):
    level = block_levels(stream_key, dims, shards, -0.22, 0.18) if shards else 1.0
    values = jax.random.normal(stream_key, dims, jnp.float32) * width * level
    return jnp.minimum(jnp.maximum(values, -limit), limit).astype(held_as)


def setup_inputs(seed: int = 0) -> dict:
    arg_keys = jax.random.split(jax.random.key(seed), 7)
    return {
        "pointing": noise(arg_keys[0], (SCANS, NS, KP), KP ** -0.5, 0.125, ((0, 8), (1, 16))),
        "ground_bin": with_ends(jax.random.randint(arg_keys[1], (SCANS, NS), 0, NGB), jax.random.fold_in(arg_keys[1], 1), 0, NGB - 1).astype(jnp.int32),
        "degrees": with_ends(jax.random.randint(arg_keys[2], (SCANS,), 2, DEG_MAX + 1), jax.random.fold_in(arg_keys[2], 1), 2, DEG_MAX).astype(jnp.int32),
        "lengths": uneven_parts(arg_keys[3], SCANS, SCANS * NS * 5 // 8, NS, 2).astype(jnp.int32),
        "tile_lists": draw_tile_lists(jax.random.fold_in(arg_keys[6], 71), 0),
        "owner_map": draw_owner_map(jax.random.fold_in(arg_keys[6], 71), 0),
    }


def build_templates(ground_row, first_row, length_one, degree_one):
    sample_rows = ground_row.shape[0]
    position = (first_row + jnp.arange(sample_rows)).astype(jnp.float32)
    length_value = length_one.astype(jnp.float32)
    inside = position < length_value
    coord = 2.0 * (position + 0.5) / length_value - 1.0
    columns = []
    previous = jnp.ones_like(coord)
    current = coord
    for degree in range(1, DEG_MAX + 1):
        keep = jnp.logical_and(inside, degree <= degree_one)
        columns.append(jnp.where(keep, current, jnp.float32(0.0)))
        following = ((2.0 * degree + 1.0) * coord * current - degree * previous) / (degree + 1.0)
        previous, current = (current, following)
    poly_part = jnp.stack(columns, axis=1)
    bins = jnp.logical_and(ground_row[:, None] == jnp.arange(NGB)[None, :], inside[:, None]).astype(jnp.float32)
    return jnp.concatenate([poly_part, bins], axis=1).astype(jnp.bfloat16)

def reference(pointing, ground_bin, degrees, lengths, tile_lists, owner_map):
    start_matrix = jnp.zeros((NTILE, TILE_PIX, NTILE, TILE_PIX), jnp.float32)

    def one_scan(matrix, inputs):
        point_one, ground_one, degree_one, length_one, tiles_one = inputs
        inside = jnp.arange(NS) < length_one
        masked = jnp.where(inside[:, None], point_one, jnp.zeros_like(point_one))
        template = build_templates(ground_one, 0, length_one, degree_one)
        masked_f = masked.astype(jnp.float32)
        template_f = template.astype(jnp.float32)
        highest = lax.Precision.HIGHEST
        gram = jnp.dot(masked_f.T, masked_f, precision=highest)
        projected = jnp.dot(template_f.T, masked_f, precision=highest)
        normal = jnp.dot(template_f.T, template_f, precision=highest) + jnp.eye(NTPL, dtype=jnp.float32)
        factor = jnp.linalg.cholesky(normal)
        whitened = jax.scipy.linalg.solve_triangular(factor, projected, lower=True)
        contrib = gram - jnp.dot(whitened.T, whitened, precision=highest)
        blocks = contrib.reshape(K, TILE_PIX, K, TILE_PIX).transpose(0, 2, 1, 3)
        row_blocks = owner_map[tiles_one] * N_SCAN + tiles_one // N_TILE
        matrix = matrix.at[row_blocks[:, None], :, tiles_one[None, :], :].add(blocks)
        return (matrix, None)
    final, unused = lax.scan(one_scan, start_matrix, (pointing, ground_bin, degrees, lengths, tile_lists))
    return final.reshape(NTILE * TILE_PIX, NTILE * TILE_PIX)
```

```python
import jax
import jax.numpy as jnp
from jax import lax
from jax.sharding import Mesh, PartitionSpec as P

DEG_MAX = 8
NGB = 24
SCAN_AXES = ("sy", "sx")


def build_templates(ground_rows, position, lengths, degrees):
    position = position.astype(jnp.float32)
    length_value = lengths.astype(jnp.float32)[:, None]
    inside = position[None, :] < length_value
    coord = 2.0 * (position[None, :] + 0.5) / length_value - 1.0
    columns = []
    previous = jnp.ones_like(coord)
    current = coord
    for degree in range(1, DEG_MAX + 1):
        keep = jnp.logical_and(inside, (degree <= degrees)[:, None])
        columns.append(jnp.where(keep, current, jnp.float32(0.0)))
        following = ((2.0 * degree + 1.0) * coord * current - degree * previous) / (degree + 1.0)
        previous, current = (current, following)
    poly_part = jnp.stack(columns, axis=2)
    bins = jnp.logical_and(
        ground_rows[:, :, None] == jnp.arange(NGB)[None, None, :], inside[:, :, None]
    ).astype(jnp.float32)
    return jnp.concatenate([poly_part, bins], axis=2).astype(jnp.bfloat16)


def per_device(pointing, ground_bin, degrees, lengths, tile_lists, owner_map):
    scan_count, sample_rows, width = pointing.shape
    n_sy = lax.axis_size("sy")
    n_sx = lax.axis_size("sx")
    n_scan = n_sy * n_sx
    n_tile = lax.axis_size("tile")
    sy = lax.axis_index("sy")
    sx = lax.axis_index("sx")
    scan_index = sy * n_sx + sx
    k_tiles = tile_lists.shape[1]
    tile_pixels = width // k_tiles
    col_width = tile_pixels
    half = k_tiles // 2 + 1
    template_cols = DEG_MAX + NGB

    position = scan_index * sample_rows + jnp.arange(sample_rows)
    inside = position[None, :] < lengths[:, None]
    masked = jnp.where(inside[:, :, None], pointing, jnp.zeros_like(pointing))
    template = build_templates(ground_bin, position, lengths, degrees)
    proj_part = jnp.einsum("snt,snp->stp", template, masked, preferred_element_type=jnp.float32)
    norm_part = jnp.einsum("snt,snu->stu", template, template, preferred_element_type=jnp.float32)
    proj, norm = lax.psum((proj_part, norm_part), SCAN_AXES)

    rows_x = lax.all_gather(masked, "sx", axis=1, tiled=True)
    wrapped = jnp.concatenate([rows_x, rows_x[:, :, : half * tile_pixels]], axis=2)
    parts = []
    for y in range(n_sy):
        col = y * n_sx + sx
        row_blocks = lax.dynamic_slice_in_dim(wrapped, col * tile_pixels, half * tile_pixels, 2)
        col_block = lax.dynamic_slice_in_dim(rows_x, col * tile_pixels, tile_pixels, 2)
        parts.append(
            jnp.einsum("snp,snq->spq", row_blocks, col_block, preferred_element_type=jnp.float32)
        )
    gram_part = lax.psum_scatter(jnp.stack(parts), "sy", scatter_dimension=0, tiled=False)

    normal = norm + jnp.eye(template_cols, dtype=jnp.float32)[None, :, :]
    factor = jnp.linalg.cholesky(normal)
    whitened = jax.scipy.linalg.solve_triangular(factor, proj, lower=True)
    w_wrapped = jnp.concatenate([whitened, whitened[:, :, : half * tile_pixels]], axis=2)
    w_rows = lax.dynamic_slice_in_dim(w_wrapped, scan_index * tile_pixels, half * tile_pixels, 2)
    w_col = lax.dynamic_slice_in_dim(whitened, scan_index * tile_pixels, tile_pixels, 2)
    correction = jnp.einsum("stp,stq->spq", w_rows, w_col, precision=lax.Precision.HIGHEST)
    own = (gram_part - correction).reshape(scan_count, half, tile_pixels, col_width)

    received = []
    for d in range(k_tiles - half, 0, -1):
        block = jnp.swapaxes(own[:, d], 1, 2)
        perm = [(i, (i + d) % n_scan) for i in range(n_scan)]
        received.append(lax.ppermute(block, SCAN_AXES, perm))
    relative = jnp.concatenate([own, jnp.stack(received, axis=1)], axis=1)
    column = jnp.roll(relative, scan_index, axis=1)
    contrib = column.reshape(scan_count, width, col_width)

    k_cols = 1
    tile_rows = contrib.reshape(scan_count * k_tiles, tile_pixels, col_width)
    row_tiles = tile_lists.reshape(-1)
    matches = row_tiles[:, None] == jnp.arange(owner_map.shape[0])[None, :]
    owners = jnp.sum(jnp.where(matches, owner_map[None, :], 0), axis=1)
    row_total = scan_count * k_tiles
    capacity = row_total // n_tile
    ordering = jnp.argsort(owners * row_total + jnp.arange(row_total), stable=True)
    local_cols = (
        lax.dynamic_slice_in_dim(tile_lists, scan_index * k_cols, k_cols, 1) - scan_index * n_tile
    )
    local_cols = jnp.repeat(local_cols, k_tiles, axis=0)
    labels = jnp.concatenate([(row_tiles // n_tile)[:, None], local_cols], axis=1)
    send_rows = tile_rows[ordering].reshape(n_tile, capacity, tile_pixels, col_width)
    send_labels = labels[ordering].reshape(n_tile, capacity, 1 + k_cols)
    recv_rows, recv_labels = (
        lax.all_to_all(send_rows, "tile", split_axis=0, concat_axis=0, tiled=True),
        lax.all_to_all(send_labels, "tile", split_axis=0, concat_axis=0, tiled=True),
    )
    item_total = n_tile * capacity
    recv_rows = recv_rows.reshape(item_total, tile_pixels, k_cols, tile_pixels)
    recv_labels = recv_labels.reshape(item_total, 1 + k_cols)
    row_select = (recv_labels[:, 0:1] == jnp.arange(n_scan)[None, :]).astype(jnp.float32)
    col_select = (recv_labels[:, 1:, None] == jnp.arange(n_tile)[None, None, :]).astype(jnp.float32)
    placing = row_select[:, :, None, None] * col_select[:, None, :, :]
    placed = jnp.einsum("irkc,ixky->rxcy", placing, recv_rows, precision=lax.Precision.HIGHEST)
    return placed.reshape(n_scan * tile_pixels, n_tile * tile_pixels)


def solution(mesh):
    devices = mesh.devices.transpose([mesh.axis_names.index("scan"), mesh.axis_names.index("tile")])
    n_scan, n_tile = devices.shape
    n_sx = 4 if n_scan % 4 == 0 else 1
    sub = Mesh(devices.reshape(n_scan // n_sx, n_sx, n_tile), ("sy", "sx", "tile"))
    return jax.shard_map(
        per_device,
        mesh=sub,
        in_specs=(
            P("tile", SCAN_AXES, None),
            P("tile", SCAN_AXES),
            P("tile"),
            P("tile"),
            P("tile", None),
            P(),
        ),
        out_specs=P("tile", SCAN_AXES),
        check_vma=False,
    )
```

```python
import jax
import jax.numpy as jnp
from jax import lax
from jax.sharding import Mesh, PartitionSpec as P

DEG_MAX = 8
NGB = 24
SCAN_AXES = ("sy", "sx")


def build_templates(ground_rows, position, lengths, degrees):
    position = position.astype(jnp.float32)
    length_value = lengths.astype(jnp.float32)[:, None]
    inside = position[None, :] < length_value
    coord = 2.0 * (position[None, :] + 0.5) / length_value - 1.0
    columns = []
    previous = jnp.ones_like(coord)
    current = coord
    for degree in range(1, DEG_MAX + 1):
        keep = jnp.logical_and(inside, (degree <= degrees)[:, None])
        columns.append(jnp.where(keep, current, jnp.float32(0.0)))
        following = ((2.0 * degree + 1.0) * coord * current - degree * previous) / (degree + 1.0)
        previous, current = (current, following)
    poly_part = jnp.stack(columns, axis=2)
    bins = jnp.logical_and(
        ground_rows[:, :, None] == jnp.arange(NGB)[None, None, :], inside[:, :, None]
    ).astype(jnp.float32)
    return jnp.concatenate([poly_part, bins], axis=2).astype(jnp.bfloat16)


def per_device(pointing, ground_bin, degrees, lengths, tile_lists, owner_map):
    scan_count, sample_rows, width = pointing.shape
    n_sy = lax.axis_size("sy")
    n_sx = lax.axis_size("sx")
    n_scan = n_sy * n_sx
    n_tile = lax.axis_size("tile")
    sy = lax.axis_index("sy")
    sx = lax.axis_index("sx")
    scan_index = sy * n_sx + sx
    k_tiles = tile_lists.shape[1]
    tile_pixels = width // k_tiles
    col_width = tile_pixels
    half = k_tiles // 2 + 1
    template_cols = DEG_MAX + NGB

    position = scan_index * sample_rows + jnp.arange(sample_rows)
    inside = position[None, :] < lengths[:, None]
    masked = jnp.where(inside[:, :, None], pointing, jnp.zeros_like(pointing))
    template = build_templates(ground_bin, position, lengths, degrees)
    local = jnp.concatenate([masked, template], axis=2)

    def column_blocks(one, gather_axis, reduce_axis, n_group):
        rows_all = lax.all_gather(one, gather_axis, axis=1, tiled=True)
        rows = rows_all[:, :, :width]
        tpl = rows_all[:, :, width:]
        wrapped = jnp.concatenate([rows, rows[:, :, : half * tile_pixels]], axis=2)
        norm = jnp.einsum("snt,snu->stu", tpl, tpl, preferred_element_type=jnp.float32)
        norm = jnp.pad(norm, ((0, 0), (0, 0), (0, col_width)))
        parts = []
        for g in range(n_group):
            col = g * n_sx + sx if reduce_axis == "sy" else sy * n_sx + g
            row_blocks = lax.dynamic_slice_in_dim(wrapped, col * tile_pixels, half * tile_pixels, 2)
            col_block = lax.dynamic_slice_in_dim(rows, col * tile_pixels, tile_pixels, 2)
            gram = jnp.einsum("snp,snq->spq", row_blocks, col_block, preferred_element_type=jnp.float32)
            proj = jnp.einsum("snp,snt->spt", row_blocks, tpl, preferred_element_type=jnp.float32)
            parts.append(jnp.concatenate([jnp.concatenate([gram, proj], axis=2), norm], axis=1))
        summed = lax.psum_scatter(jnp.stack(parts), reduce_axis, scatter_dimension=0, tiled=False)
        gram = summed[:, : half * tile_pixels, :col_width]
        proj = jnp.swapaxes(summed[:, : half * tile_pixels, col_width:], 1, 2)
        normal = summed[:, half * tile_pixels :, :template_cols]
        normal = normal + jnp.eye(template_cols, dtype=jnp.float32)[None, :, :]
        factor = jnp.linalg.cholesky(normal)
        whitened = jax.scipy.linalg.solve_triangular(factor, proj, lower=True)
        correction = jnp.einsum(
            "stp,stq->spq", whitened, whitened[:, :, :tile_pixels], precision=lax.Precision.HIGHEST
        )
        return gram - correction

    own = jnp.concatenate(
        [
            column_blocks(local[0:1], "sx", "sy", n_sy),
            column_blocks(local[1:2], "sy", "sx", n_sx),
        ],
        axis=0,
    ).reshape(scan_count, half, tile_pixels, col_width)

    received = []
    for d in range(k_tiles - half, 0, -1):
        block = jnp.swapaxes(own[:, d], 1, 2)
        perm = [(i, (i + d) % n_scan) for i in range(n_scan)]
        received.append(lax.ppermute(block, SCAN_AXES, perm))
    relative = jnp.concatenate([own, jnp.stack(received, axis=1)], axis=1)
    column = jnp.roll(relative, scan_index, axis=1)
    contrib = column.reshape(scan_count, width, col_width)

    k_cols = 1
    tile_rows = contrib.reshape(scan_count * k_tiles, tile_pixels, col_width)
    row_tiles = tile_lists.reshape(-1)
    matches = row_tiles[:, None] == jnp.arange(owner_map.shape[0])[None, :]
    owners = jnp.sum(jnp.where(matches, owner_map[None, :], 0), axis=1)
    row_total = scan_count * k_tiles
    capacity = row_total // n_tile
    ordering = jnp.argsort(owners * row_total + jnp.arange(row_total), stable=True)
    local_cols = (
        lax.dynamic_slice_in_dim(tile_lists, scan_index * k_cols, k_cols, 1) - scan_index * n_tile
    )
    local_cols = jnp.repeat(local_cols, k_tiles, axis=0)
    labels = jnp.concatenate([(row_tiles // n_tile)[:, None], local_cols], axis=1)
    send_rows = tile_rows[ordering].reshape(n_tile, capacity, tile_pixels, col_width)
    send_labels = labels[ordering].reshape(n_tile, capacity, 1 + k_cols)
    recv_rows, recv_labels = (
        lax.all_to_all(send_rows, "tile", split_axis=0, concat_axis=0, tiled=True),
        lax.all_to_all(send_labels, "tile", split_axis=0, concat_axis=0, tiled=True),
    )
    item_total = n_tile * capacity
    recv_rows = recv_rows.reshape(item_total, tile_pixels, k_cols, tile_pixels)
    recv_labels = recv_labels.reshape(item_total, 1 + k_cols)
    row_select = (recv_labels[:, 0:1] == jnp.arange(n_scan)[None, :]).astype(jnp.float32)
    col_select = (recv_labels[:, 1:, None] == jnp.arange(n_tile)[None, None, :]).astype(jnp.float32)
    placing = row_select[:, :, None, None] * col_select[:, None, :, :]
    placed = jnp.einsum("irkc,ixky->rxcy", placing, recv_rows, precision=lax.Precision.HIGHEST)
    return placed.reshape(n_scan * tile_pixels, n_tile * tile_pixels)


def solution(mesh):
    devices = mesh.devices.transpose([mesh.axis_names.index("scan"), mesh.axis_names.index("tile")])
    n_scan, n_tile = devices.shape
    n_sx = 4 if n_scan % 4 == 0 else 1
    sub = Mesh(devices.reshape(n_scan // n_sx, n_sx, n_tile), ("sy", "sx", "tile"))
    return jax.shard_map(
        per_device,
        mesh=sub,
        in_specs=(
            P("tile", SCAN_AXES, None),
            P("tile", SCAN_AXES),
            P("tile"),
            P("tile"),
            P("tile", None),
            P(),
        ),
        out_specs=P("tile", SCAN_AXES),
        check_vma=False,
    )
```

```python
import jax
import jax.numpy as jnp
from jax import lax
from jax.sharding import Mesh, PartitionSpec as P

DEG_MAX = 8
NGB = 24
SCAN_AXES = ("sy", "sx")


def build_templates(ground_rows, position, lengths, degrees):
    position = position.astype(jnp.float32)
    length_value = lengths.astype(jnp.float32)[:, None]
    inside = position[None, :] < length_value
    coord = 2.0 * (position[None, :] + 0.5) / length_value - 1.0
    columns = []
    previous = jnp.ones_like(coord)
    current = coord
    for degree in range(1, DEG_MAX + 1):
        keep = jnp.logical_and(inside, (degree <= degrees)[:, None])
        columns.append(jnp.where(keep, current, jnp.float32(0.0)))
        following = ((2.0 * degree + 1.0) * coord * current - degree * previous) / (degree + 1.0)
        previous, current = (current, following)
    poly_part = jnp.stack(columns, axis=2)
    bins = jnp.logical_and(
        ground_rows[:, :, None] == jnp.arange(NGB)[None, None, :], inside[:, :, None]
    ).astype(jnp.float32)
    return jnp.concatenate([poly_part, bins], axis=2).astype(jnp.bfloat16)


def per_device(pointing, ground_bin, degrees, lengths, tile_lists, owner_map):
    scan_count, sample_rows, width = pointing.shape
    n_sy = lax.axis_size("sy")
    n_sx = lax.axis_size("sx")
    n_scan = n_sy * n_sx
    n_tile = lax.axis_size("tile")
    sy = lax.axis_index("sy")
    sx = lax.axis_index("sx")
    scan_index = sy * n_sx + sx
    k_tiles = tile_lists.shape[1]
    tile_pixels = width // k_tiles
    col_width = tile_pixels
    half = k_tiles // 2 + 1
    template_cols = DEG_MAX + NGB

    position = scan_index * sample_rows + jnp.arange(sample_rows)
    inside = position[None, :] < lengths[:, None]
    masked = jnp.where(inside[:, :, None], pointing, jnp.zeros_like(pointing))
    template = build_templates(ground_bin, position, lengths, degrees)
    local = jnp.concatenate([masked, template], axis=2)

    def shifted(x, axis, n, d):
        return lax.ppermute(x, axis, [(i, (i + d) % n) for i in range(n)])

    rows_all = jnp.concatenate(
        [local] + [shifted(local, "sx", n_sx, d) for d in range(1, n_sx)], axis=1
    )
    rows = rows_all[:, :, :width]
    tpl = rows_all[:, :, width:]
    wrapped = jnp.concatenate([rows, rows[:, :, : half * tile_pixels]], axis=2)
    norm = jnp.einsum("snt,snu->stu", tpl, tpl, preferred_element_type=jnp.float32)
    norm = jnp.pad(norm, ((0, 0), (0, 0), (0, col_width)))

    summed = None
    for d in range(n_sy):
        col = ((sy + d) % n_sy) * n_sx + sx
        row_blocks = lax.dynamic_slice_in_dim(wrapped, col * tile_pixels, half * tile_pixels, 2)
        col_block = lax.dynamic_slice_in_dim(rows, col * tile_pixels, tile_pixels, 2)
        gram = jnp.einsum("snp,snq->spq", row_blocks, col_block, preferred_element_type=jnp.float32)
        proj = jnp.einsum("snp,snt->spt", row_blocks, tpl, preferred_element_type=jnp.float32)
        part = jnp.concatenate([jnp.concatenate([gram, proj], axis=2), norm], axis=1)
        part = part if d == 0 else shifted(part, "sy", n_sy, d)
        summed = part if summed is None else summed + part

    gram = summed[:, : half * tile_pixels, :col_width]
    proj = jnp.swapaxes(summed[:, : half * tile_pixels, col_width:], 1, 2)
    normal = summed[:, half * tile_pixels :, :template_cols]
    normal = normal + jnp.eye(template_cols, dtype=jnp.float32)[None, :, :]
    factor = jnp.linalg.cholesky(normal)
    whitened = jax.scipy.linalg.solve_triangular(factor, proj, lower=True)
    correction = jnp.einsum(
        "stp,stq->spq", whitened, whitened[:, :, :tile_pixels], precision=lax.Precision.HIGHEST
    )
    own = (gram - correction).reshape(scan_count, half, tile_pixels, col_width)

    received = []
    for d in range(k_tiles - half, 0, -1):
        block = jnp.swapaxes(own[:, d], 1, 2)
        perm = [(i, (i + d) % n_scan) for i in range(n_scan)]
        received.append(lax.ppermute(block, SCAN_AXES, perm))
    relative = jnp.concatenate([own, jnp.stack(received, axis=1)], axis=1)
    column = jnp.roll(relative, scan_index, axis=1)
    contrib = column.reshape(scan_count, width, col_width)

    k_cols = 1
    tile_rows = contrib.reshape(scan_count * k_tiles, tile_pixels, col_width)
    row_tiles = tile_lists.reshape(-1)
    matches = row_tiles[:, None] == jnp.arange(owner_map.shape[0])[None, :]
    owners = jnp.sum(jnp.where(matches, owner_map[None, :], 0), axis=1)
    row_total = scan_count * k_tiles
    capacity = row_total // n_tile
    ordering = jnp.argsort(owners * row_total + jnp.arange(row_total), stable=True)
    local_cols = (
        lax.dynamic_slice_in_dim(tile_lists, scan_index * k_cols, k_cols, 1) - scan_index * n_tile
    )
    local_cols = jnp.repeat(local_cols, k_tiles, axis=0)
    labels = jnp.concatenate([(row_tiles // n_tile)[:, None], local_cols], axis=1)
    send_rows = tile_rows[ordering].reshape(n_tile, capacity, tile_pixels, col_width)
    send_labels = labels[ordering].reshape(n_tile, capacity, 1 + k_cols)
    recv_rows, recv_labels = (
        lax.all_to_all(send_rows, "tile", split_axis=0, concat_axis=0, tiled=True),
        lax.all_to_all(send_labels, "tile", split_axis=0, concat_axis=0, tiled=True),
    )
    item_total = n_tile * capacity
    recv_rows = recv_rows.reshape(item_total, tile_pixels, k_cols, tile_pixels)
    recv_labels = recv_labels.reshape(item_total, 1 + k_cols)
    row_select = (recv_labels[:, 0:1] == jnp.arange(n_scan)[None, :]).astype(jnp.float32)
    col_select = (recv_labels[:, 1:, None] == jnp.arange(n_tile)[None, None, :]).astype(jnp.float32)
    placing = row_select[:, :, None, None] * col_select[:, None, :, :]
    placed = jnp.einsum("irkc,ixky->rxcy", placing, recv_rows, precision=lax.Precision.HIGHEST)
    return placed.reshape(n_scan * tile_pixels, n_tile * tile_pixels)


def solution(mesh):
    devices = mesh.devices.transpose([mesh.axis_names.index("scan"), mesh.axis_names.index("tile")])
    n_scan, n_tile = devices.shape
    n_sx = 4 if n_scan % 4 == 0 else 1
    sub = Mesh(devices.reshape(n_scan // n_sx, n_sx, n_tile), ("sy", "sx", "tile"))
    return jax.shard_map(
        per_device,
        mesh=sub,
        in_specs=(
            P("tile", SCAN_AXES, None),
            P("tile", SCAN_AXES),
            P("tile"),
            P("tile"),
            P("tile", None),
            P(),
        ),
        out_specs=P("tile", SCAN_AXES),
        check_vma=False,
    )
```

```python
import jax
import jax.numpy as jnp
from jax import lax
from jax.sharding import Mesh, PartitionSpec as P

DEG_MAX = 8
NGB = 24
SCAN_AXES = ("sy", "sx")


def build_templates(ground_rows, position, lengths, degrees):
    position = position.astype(jnp.float32)
    length_value = lengths.astype(jnp.float32)[:, None]
    inside = position[None, :] < length_value
    coord = 2.0 * (position[None, :] + 0.5) / length_value - 1.0
    columns = []
    previous = jnp.ones_like(coord)
    current = coord
    for degree in range(1, DEG_MAX + 1):
        keep = jnp.logical_and(inside, (degree <= degrees)[:, None])
        columns.append(jnp.where(keep, current, jnp.float32(0.0)))
        following = ((2.0 * degree + 1.0) * coord * current - degree * previous) / (degree + 1.0)
        previous, current = (current, following)
    poly_part = jnp.stack(columns, axis=2)
    bins = jnp.logical_and(
        ground_rows[:, :, None] == jnp.arange(NGB)[None, None, :], inside[:, :, None]
    ).astype(jnp.float32)
    return jnp.concatenate([poly_part, bins], axis=2).astype(jnp.bfloat16)


def per_device(pointing, ground_bin, degrees, lengths, tile_lists, owner_map):
    scan_count, sample_rows, width = pointing.shape
    n_sy = lax.axis_size("sy")
    n_sx = lax.axis_size("sx")
    n_scan = n_sy * n_sx
    n_tile = lax.axis_size("tile")
    sy = lax.axis_index("sy")
    sx = lax.axis_index("sx")
    scan_index = sy * n_sx + sx
    k_tiles = tile_lists.shape[1]
    tile_pixels = width // k_tiles
    col_width = tile_pixels
    half = k_tiles // 2 + 1
    template_cols = DEG_MAX + NGB

    position = scan_index * sample_rows + jnp.arange(sample_rows)
    inside = position[None, :] < lengths[:, None]
    masked = jnp.where(inside[:, :, None], pointing, jnp.zeros_like(pointing))
    template = build_templates(ground_bin, position, lengths, degrees)
    local = jnp.concatenate([masked, template], axis=2)

    def shifted(x, axis, n, d):
        return lax.ppermute(x, axis, [(i, (i + d) % n) for i in range(n)])

    def column_blocks(one, gather_axis, n_gather, reduce_axis, n_reduce, reduce_index):
        rows_all = jnp.concatenate(
            [one] + [shifted(one, gather_axis, n_gather, d) for d in range(1, n_gather)], axis=1
        )
        rows = rows_all[:, :, :width]
        tpl = rows_all[:, :, width:]
        grid = rows.reshape(1, rows.shape[1], n_sy, n_sx, tile_pixels)
        if reduce_axis == "sy":
            cols = lax.dynamic_index_in_dim(grid, sx, 3, keepdims=False)
            firsts = [g * n_sx + sx for g in range(n_reduce)]
        else:
            cols = lax.dynamic_index_in_dim(grid, sy, 2, keepdims=False)
            firsts = [sy * n_sx + g for g in range(n_reduce)]
        grams = jnp.einsum("snp,sngq->sgpq", rows, cols, preferred_element_type=jnp.float32)
        projs = jnp.einsum("snp,snt->spt", rows, tpl, preferred_element_type=jnp.float32)
        norm = jnp.einsum("snt,snu->stu", tpl, tpl, preferred_element_type=jnp.float32)
        norm = jnp.pad(norm, ((0, 0), (0, 0), (0, col_width)))
        both = jnp.concatenate(
            [grams, jnp.broadcast_to(projs[:, None], (1, n_reduce) + projs.shape[1:])], axis=3
        )
        both = jnp.concatenate([both, both[:, :, : half * tile_pixels]], axis=2)
        payloads = []
        for g in range(n_reduce):
            slab = lax.dynamic_slice_in_dim(both[:, g], firsts[g] * tile_pixels, half * tile_pixels, 1)
            payloads.append(jnp.concatenate([slab, norm], axis=1))
        payloads = jnp.stack(payloads)
        summed = None
        for d in range(n_reduce):
            part = lax.dynamic_index_in_dim(payloads, (reduce_index + d) % n_reduce, 0, keepdims=False)
            part = part if d == 0 else shifted(part, reduce_axis, n_reduce, d)
            summed = part if summed is None else summed + part
        gram = summed[:, : half * tile_pixels, :col_width]
        proj = jnp.swapaxes(summed[:, : half * tile_pixels, col_width:], 1, 2)
        normal = summed[:, half * tile_pixels :, :template_cols]
        normal = normal + jnp.eye(template_cols, dtype=jnp.float32)[None, :, :]
        factor = jnp.linalg.cholesky(normal)
        whitened = jax.scipy.linalg.solve_triangular(factor, proj, lower=True)
        correction = jnp.einsum(
            "stp,stq->spq", whitened, whitened[:, :, :tile_pixels], precision=lax.Precision.HIGHEST
        )
        return gram - correction

    own = jnp.concatenate(
        [
            column_blocks(local[0:1], "sx", n_sx, "sy", n_sy, sy),
            column_blocks(local[1:2], "sy", n_sy, "sx", n_sx, sx),
        ],
        axis=0,
    ).reshape(scan_count, half, tile_pixels, col_width)

    received = []
    for d in range(k_tiles - half, 0, -1):
        block = jnp.swapaxes(own[:, d], 1, 2)
        perm = [(i, (i + d) % n_scan) for i in range(n_scan)]
        received.append(lax.ppermute(block, SCAN_AXES, perm))
    relative = jnp.concatenate([own, jnp.stack(received, axis=1)], axis=1)
    column = jnp.roll(relative, scan_index, axis=1)
    contrib = column.reshape(scan_count, width, col_width)

    k_cols = 1
    tile_rows = contrib.reshape(scan_count * k_tiles, tile_pixels, col_width)
    row_tiles = tile_lists.reshape(-1)
    matches = row_tiles[:, None] == jnp.arange(owner_map.shape[0])[None, :]
    owners = jnp.sum(jnp.where(matches, owner_map[None, :], 0), axis=1)
    row_total = scan_count * k_tiles
    capacity = row_total // n_tile
    ordering = jnp.argsort(owners * row_total + jnp.arange(row_total), stable=True)
    local_cols = (
        lax.dynamic_slice_in_dim(tile_lists, scan_index * k_cols, k_cols, 1) - scan_index * n_tile
    )
    local_cols = jnp.repeat(local_cols, k_tiles, axis=0)
    labels = jnp.concatenate([(row_tiles // n_tile)[:, None], local_cols], axis=1)
    send_rows = tile_rows[ordering].reshape(n_tile, capacity, tile_pixels, col_width)
    send_labels = labels[ordering].reshape(n_tile, capacity, 1 + k_cols)
    recv_rows, recv_labels = (
        lax.all_to_all(send_rows, "tile", split_axis=0, concat_axis=0, tiled=True),
        lax.all_to_all(send_labels, "tile", split_axis=0, concat_axis=0, tiled=True),
    )
    item_total = n_tile * capacity
    recv_rows = recv_rows.reshape(item_total, tile_pixels, k_cols, tile_pixels)
    recv_labels = recv_labels.reshape(item_total, 1 + k_cols)
    row_select = (recv_labels[:, 0:1] == jnp.arange(n_scan)[None, :]).astype(jnp.float32)
    col_select = (recv_labels[:, 1:, None] == jnp.arange(n_tile)[None, None, :]).astype(jnp.float32)
    placing = row_select[:, :, None, None] * col_select[:, None, :, :]
    placed = jnp.einsum("irkc,ixky->rxcy", placing, recv_rows, precision=lax.Precision.HIGHEST)
    return placed.reshape(n_scan * tile_pixels, n_tile * tile_pixels)


def solution(mesh):
    devices = mesh.devices.transpose([mesh.axis_names.index("scan"), mesh.axis_names.index("tile")])
    n_scan, n_tile = devices.shape
    n_sx = 4 if n_scan % 4 == 0 else 1
    sub = Mesh(devices.reshape(n_scan // n_sx, n_sx, n_tile), ("sy", "sx", "tile"))
    return jax.shard_map(
        per_device,
        mesh=sub,
        in_specs=(
            P("tile", SCAN_AXES, None),
            P("tile", SCAN_AXES),
            P("tile"),
            P("tile"),
            P("tile", None),
            P(),
        ),
        out_specs=P("tile", SCAN_AXES),
        check_vma=False,
    )
```

```python
import jax
import jax.numpy as jnp
from jax import lax
from jax.sharding import Mesh, PartitionSpec as P

DEG_MAX = 8
NGB = 24
SCAN_AXES = ("sy", "sx")


def build_templates(ground_rows, position, lengths, degrees):
    position = position.astype(jnp.float32)
    length_value = lengths.astype(jnp.float32)[:, None]
    inside = position[None, :] < length_value
    coord = 2.0 * (position[None, :] + 0.5) / length_value - 1.0
    columns = []
    previous = jnp.ones_like(coord)
    current = coord
    for degree in range(1, DEG_MAX + 1):
        keep = jnp.logical_and(inside, (degree <= degrees)[:, None])
        columns.append(jnp.where(keep, current, jnp.float32(0.0)))
        following = ((2.0 * degree + 1.0) * coord * current - degree * previous) / (degree + 1.0)
        previous, current = (current, following)
    poly_part = jnp.stack(columns, axis=2)
    bins = jnp.logical_and(
        ground_rows[:, :, None] == jnp.arange(NGB)[None, None, :], inside[:, :, None]
    ).astype(jnp.float32)
    return jnp.concatenate([poly_part, bins], axis=2).astype(jnp.bfloat16)


def per_device(pointing, ground_bin, degrees, lengths, tile_lists, owner_map):
    scan_count, sample_rows, width = pointing.shape
    n_sy = lax.axis_size("sy")
    n_sx = lax.axis_size("sx")
    n_scan = n_sy * n_sx
    n_tile = lax.axis_size("tile")
    sy = lax.axis_index("sy")
    sx = lax.axis_index("sx")
    scan_index = sy * n_sx + sx
    k_tiles = tile_lists.shape[1]
    tile_pixels = width // k_tiles
    col_width = tile_pixels
    half = k_tiles // 2 + 1
    template_cols = DEG_MAX + NGB

    position = scan_index * sample_rows + jnp.arange(sample_rows)
    inside = position[None, :] < lengths[:, None]
    masked = jnp.where(inside[:, :, None], pointing, jnp.zeros_like(pointing))
    template = build_templates(ground_bin, position, lengths, degrees)

    def shifted(x, axis, n, d):
        return lax.ppermute(x, axis, [(i, (i + d) % n) for i in range(n)])

    def column_blocks(one, one_tpl, gather_axis, n_gather, reduce_axis, n_reduce, reduce_index):
        moved = [shifted((one, one_tpl), gather_axis, n_gather, d) for d in range(1, n_gather)]
        rows = jnp.concatenate([one] + [m[0] for m in moved], axis=1)
        tpl = jnp.concatenate([one_tpl] + [m[1] for m in moved], axis=1)
        if reduce_axis == "sy":
            firsts = [g * n_sx + sx for g in range(n_reduce)]
        else:
            firsts = [sy * n_sx + g for g in range(n_reduce)]
        cols = jnp.concatenate(
            [lax.dynamic_slice_in_dim(rows, f * tile_pixels, tile_pixels, 2) for f in firsts], axis=2
        )
        grams = jnp.einsum("snp,snq->spq", rows, cols, preferred_element_type=jnp.float32)
        grams = grams.reshape(k_tiles, tile_pixels, n_reduce, col_width)
        projs = jnp.einsum("snt,snp->stp", tpl, rows, preferred_element_type=jnp.float32)
        projs = projs.reshape(template_cols, k_tiles, tile_pixels)
        norm = jnp.einsum("snt,snu->tu", tpl, tpl, preferred_element_type=jnp.float32)
        norm = jnp.pad(norm, ((0, 0), (0, col_width - template_cols)))
        steps = jnp.arange(half)
        payloads = []
        for g in range(n_reduce):
            picks = (firsts[g] + steps) % k_tiles
            slab = jnp.take(grams[:, :, g], picks, axis=0).reshape(half * tile_pixels, col_width)
            proj_slab = jnp.swapaxes(jnp.take(projs, picks, axis=1), 0, 1)
            proj_slab = proj_slab.reshape(half * template_cols, tile_pixels)
            payloads.append(jnp.concatenate([slab, proj_slab, norm], axis=0))
        payloads = jnp.stack(payloads)
        summed = None
        for d in range(n_reduce):
            part = lax.dynamic_index_in_dim(payloads, (reduce_index + d) % n_reduce, 0, keepdims=False)
            part = part if d == 0 else shifted(part, reduce_axis, n_reduce, d)
            summed = part if summed is None else summed + part
        split = half * tile_pixels
        gram = summed[:split]
        proj = summed[split : split + half * template_cols].reshape(half, template_cols, tile_pixels)
        proj = jnp.swapaxes(proj, 0, 1).reshape(template_cols, split)
        normal = summed[split + half * template_cols :, :template_cols]
        normal = normal + jnp.eye(template_cols, dtype=jnp.float32)
        factor = jnp.linalg.cholesky(normal)
        whitened = jax.scipy.linalg.solve_triangular(factor, proj, lower=True)
        correction = jnp.einsum(
            "tp,tq->pq", whitened, whitened[:, :tile_pixels], precision=lax.Precision.HIGHEST
        )
        return (gram - correction)[None]

    own = jnp.concatenate(
        [
            column_blocks(masked[0:1], template[0:1], "sx", n_sx, "sy", n_sy, sy),
            column_blocks(masked[1:2], template[1:2], "sy", n_sy, "sx", n_sx, sx),
        ],
        axis=0,
    ).reshape(scan_count, half, tile_pixels, col_width)

    received = []
    for d in range(k_tiles - half, 0, -1):
        block = jnp.swapaxes(own[:, d], 1, 2)
        perm = [(i, (i + d) % n_scan) for i in range(n_scan)]
        received.append(lax.ppermute(block, SCAN_AXES, perm))
    relative = jnp.concatenate([own, jnp.stack(received, axis=1)], axis=1)
    column = jnp.roll(relative, scan_index, axis=1)
    contrib = column.reshape(scan_count, width, col_width)

    k_cols = 1
    tile_rows = contrib.reshape(scan_count * k_tiles, tile_pixels, col_width)
    row_tiles = tile_lists.reshape(-1)
    matches = row_tiles[:, None] == jnp.arange(owner_map.shape[0])[None, :]
    owners = jnp.sum(jnp.where(matches, owner_map[None, :], 0), axis=1)
    row_total = scan_count * k_tiles
    capacity = row_total // n_tile
    ordering = jnp.argsort(owners * row_total + jnp.arange(row_total), stable=True)
    local_cols = (
        lax.dynamic_slice_in_dim(tile_lists, scan_index * k_cols, k_cols, 1) - scan_index * n_tile
    )
    local_cols = jnp.repeat(local_cols, k_tiles, axis=0)
    labels = jnp.concatenate([(row_tiles // n_tile)[:, None], local_cols], axis=1)
    send_rows = tile_rows[ordering].reshape(n_tile, capacity, tile_pixels, col_width)
    send_labels = labels[ordering].reshape(n_tile, capacity, 1 + k_cols)
    recv_rows, recv_labels = (
        lax.all_to_all(send_rows, "tile", split_axis=0, concat_axis=0, tiled=True),
        lax.all_to_all(send_labels, "tile", split_axis=0, concat_axis=0, tiled=True),
    )
    item_total = n_tile * capacity
    recv_rows = recv_rows.reshape(item_total, tile_pixels, k_cols, tile_pixels)
    recv_labels = recv_labels.reshape(item_total, 1 + k_cols)
    row_select = (recv_labels[:, 0:1] == jnp.arange(n_scan)[None, :]).astype(jnp.float32)
    col_select = (recv_labels[:, 1:, None] == jnp.arange(n_tile)[None, None, :]).astype(jnp.float32)
    placing = row_select[:, :, None, None] * col_select[:, None, :, :]
    placed = jnp.einsum("irkc,ixky->rxcy", placing, recv_rows, precision=lax.Precision.HIGHEST)
    return placed.reshape(n_scan * tile_pixels, n_tile * tile_pixels)


def solution(mesh):
    devices = mesh.devices.transpose([mesh.axis_names.index("scan"), mesh.axis_names.index("tile")])
    n_scan, n_tile = devices.shape
    n_sx = 4 if n_scan % 4 == 0 else 1
    sub = Mesh(devices.reshape(n_scan // n_sx, n_sx, n_tile), ("sy", "sx", "tile"))
    return jax.shard_map(
        per_device,
        mesh=sub,
        in_specs=(
            P("tile", SCAN_AXES, None),
            P("tile", SCAN_AXES),
            P("tile"),
            P("tile"),
            P("tile", None),
            P(),
        ),
        out_specs=P("tile", SCAN_AXES),
        check_vma=False,
    )
```

```python
import jax
import jax.numpy as jnp
from jax import lax
from jax.sharding import Mesh, PartitionSpec as P

DEG_MAX = 8
NGB = 24
SCAN_AXES = ("sy", "sx")


def build_templates(ground_rows, position, lengths, degrees):
    position = position.astype(jnp.float32)
    length_value = lengths.astype(jnp.float32)[:, None]
    inside = position[None, :] < length_value
    coord = 2.0 * (position[None, :] + 0.5) / length_value - 1.0
    columns = []
    previous = jnp.ones_like(coord)
    current = coord
    for degree in range(1, DEG_MAX + 1):
        keep = jnp.logical_and(inside, (degree <= degrees)[:, None])
        columns.append(jnp.where(keep, current, jnp.float32(0.0)))
        following = ((2.0 * degree + 1.0) * coord * current - degree * previous) / (degree + 1.0)
        previous, current = (current, following)
    poly_part = jnp.stack(columns, axis=2)
    bins = jnp.logical_and(
        ground_rows[:, :, None] == jnp.arange(NGB)[None, None, :], inside[:, :, None]
    ).astype(jnp.float32)
    return jnp.concatenate([poly_part, bins], axis=2).astype(jnp.bfloat16)


def per_device(pointing, ground_bin, degrees, lengths, tile_lists, owner_map):
    scan_count, sample_rows, width = pointing.shape
    n_sy = lax.axis_size("sy")
    n_sx = lax.axis_size("sx")
    n_scan = n_sy * n_sx
    n_tile = lax.axis_size("tile")
    sy = lax.axis_index("sy")
    sx = lax.axis_index("sx")
    scan_index = sy * n_sx + sx
    k_tiles = tile_lists.shape[1]
    tile_pixels = width // k_tiles
    col_width = tile_pixels
    half = k_tiles // 2 + 1
    template_cols = DEG_MAX + NGB

    position = scan_index * sample_rows + jnp.arange(sample_rows)
    inside = position[None, :] < lengths[:, None]
    masked = jnp.where(inside[:, :, None], pointing, jnp.zeros_like(pointing))
    template = build_templates(ground_bin, position, lengths, degrees)

    def shifted(x, axis, n, d):
        return lax.ppermute(x, axis, [(i, (i + d) % n) for i in range(n)])

    def column_blocks(one, one_tpl, gather_axis, n_gather, gather_index, step, reduce_axis, n_reduce, reduce_index):
        def rolled(x, d):
            offset = ((gather_index + d) % n_gather) * step * tile_pixels
            return jnp.roll(x, -offset, axis=2)

        moved = [
            shifted((rolled(one, d), one_tpl), gather_axis, n_gather, d) for d in range(1, n_gather)
        ]
        rows = jnp.concatenate([rolled(one, 0)] + [m[0] for m in moved], axis=1)
        tpl = jnp.concatenate([one_tpl] + [m[1] for m in moved], axis=1)
        stride = n_sx if reduce_axis == "sy" else 1
        firsts = [g * stride for g in range(n_reduce)]
        cols = jnp.concatenate(
            [rows[:, :, f * tile_pixels : (f + 1) * tile_pixels] for f in firsts], axis=2
        )
        grams = jnp.einsum("snp,snq->pq", rows, cols, preferred_element_type=jnp.float32)
        grams = grams.reshape(k_tiles, tile_pixels, n_reduce, col_width)
        projs = jnp.einsum("snt,snp->tp", tpl, rows, preferred_element_type=jnp.float32)
        projs = projs.reshape(template_cols, k_tiles, tile_pixels)
        norm = jnp.einsum("snt,snu->tu", tpl, tpl, preferred_element_type=jnp.float32)
        norm = jnp.pad(norm, ((0, 0), (0, col_width - template_cols)))

        def wrap_take(x, first, axis):
            x = jnp.concatenate([x, lax.slice_in_dim(x, 0, half, axis=axis)], axis=axis)
            return lax.slice_in_dim(x, first, first + half, axis=axis)

        payloads = []
        for g, f in enumerate(firsts):
            slab = wrap_take(grams[:, :, g], f, 0).reshape(half * tile_pixels, col_width)
            proj_slab = jnp.swapaxes(wrap_take(projs, f, 1), 0, 1)
            proj_slab = proj_slab.reshape(half * template_cols, tile_pixels)
            payloads.append(jnp.concatenate([slab, proj_slab, norm], axis=0))
        payloads = jnp.stack(payloads)
        summed = None
        for d in range(n_reduce):
            part = lax.dynamic_index_in_dim(payloads, (reduce_index + d) % n_reduce, 0, keepdims=False)
            part = part if d == 0 else shifted(part, reduce_axis, n_reduce, d)
            summed = part if summed is None else summed + part
        return summed

    summed = jnp.stack(
        [
            column_blocks(masked[0:1], template[0:1], "sx", n_sx, sx, 1, "sy", n_sy, sy),
            column_blocks(masked[1:2], template[1:2], "sy", n_sy, sy, n_sx, "sx", n_sx, sx),
        ]
    )
    split = half * tile_pixels
    gram = summed[:, :split]
    proj = summed[:, split : split + half * template_cols].reshape(scan_count, half, template_cols, tile_pixels)
    proj = jnp.swapaxes(proj, 1, 2).reshape(scan_count, template_cols, split)
    normal = summed[:, split + half * template_cols :, :template_cols]
    normal = normal + jnp.eye(template_cols, dtype=jnp.float32)[None]
    factor = jnp.linalg.cholesky(normal)
    whitened = jax.scipy.linalg.solve_triangular(factor, proj, lower=True)
    correction = jnp.einsum(
        "stp,stq->spq", whitened, whitened[:, :, :tile_pixels], precision=lax.Precision.HIGHEST
    )
    own = (gram - correction).reshape(scan_count, half, tile_pixels, col_width)

    received = []
    for d in range(k_tiles - half, 0, -1):
        block = jnp.swapaxes(own[:, d], 1, 2)
        perm = [(i, (i + d) % n_scan) for i in range(n_scan)]
        received.append(lax.ppermute(block, SCAN_AXES, perm))
    relative = jnp.concatenate([own, jnp.stack(received, axis=1)], axis=1)
    column = jnp.roll(relative, scan_index, axis=1)
    contrib = column.reshape(scan_count, width, col_width)

    k_cols = 1
    tile_rows = contrib.reshape(scan_count * k_tiles, tile_pixels, col_width)
    row_tiles = tile_lists.reshape(-1)
    matches = row_tiles[:, None] == jnp.arange(owner_map.shape[0])[None, :]
    owners = jnp.sum(jnp.where(matches, owner_map[None, :], 0), axis=1)
    row_total = scan_count * k_tiles
    capacity = row_total // n_tile
    ordering = jnp.argsort(owners * row_total + jnp.arange(row_total), stable=True)
    local_cols = (
        lax.dynamic_slice_in_dim(tile_lists, scan_index * k_cols, k_cols, 1) - scan_index * n_tile
    )
    local_cols = jnp.repeat(local_cols, k_tiles, axis=0)
    labels = jnp.concatenate([(row_tiles // n_tile)[:, None], local_cols], axis=1)
    send_rows = tile_rows[ordering].reshape(n_tile, capacity, tile_pixels, col_width)
    send_labels = labels[ordering].reshape(n_tile, capacity, 1 + k_cols)
    recv_rows, recv_labels = (
        lax.all_to_all(send_rows, "tile", split_axis=0, concat_axis=0, tiled=True),
        lax.all_to_all(send_labels, "tile", split_axis=0, concat_axis=0, tiled=True),
    )
    item_total = n_tile * capacity
    recv_rows = recv_rows.reshape(item_total, tile_pixels, k_cols, tile_pixels)
    recv_labels = recv_labels.reshape(item_total, 1 + k_cols)
    row_select = (recv_labels[:, 0:1] == jnp.arange(n_scan)[None, :]).astype(jnp.float32)
    col_select = (recv_labels[:, 1:, None] == jnp.arange(n_tile)[None, None, :]).astype(jnp.float32)
    placing = row_select[:, :, None, None] * col_select[:, None, :, :]
    placed = jnp.einsum("irkc,ixky->rxcy", placing, recv_rows, precision=lax.Precision.HIGHEST)
    return placed.reshape(n_scan * tile_pixels, n_tile * tile_pixels)


def solution(mesh):
    devices = mesh.devices.transpose([mesh.axis_names.index("scan"), mesh.axis_names.index("tile")])
    n_scan, n_tile = devices.shape
    n_sx = 4 if n_scan % 4 == 0 else 1
    sub = Mesh(devices.reshape(n_scan // n_sx, n_sx, n_tile), ("sy", "sx", "tile"))
    return jax.shard_map(
        per_device,
        mesh=sub,
        in_specs=(
            P("tile", SCAN_AXES, None),
            P("tile", SCAN_AXES),
            P("tile"),
            P("tile"),
            P("tile", None),
            P(),
        ),
        out_specs=P("tile", SCAN_AXES),
        check_vma=False,
    )
```

```python
import jax
import jax.numpy as jnp
from jax import lax
from jax.sharding import Mesh, PartitionSpec as P

DEG_MAX = 8
NGB = 24
SCAN_AXES = ("sy", "sx")


def build_templates(ground_rows, position, lengths, degrees):
    position = position.astype(jnp.float32)
    length_value = lengths.astype(jnp.float32)[:, None]
    inside = position[None, :] < length_value
    coord = 2.0 * (position[None, :] + 0.5) / length_value - 1.0
    columns = []
    previous = jnp.ones_like(coord)
    current = coord
    for degree in range(1, DEG_MAX + 1):
        keep = jnp.logical_and(inside, (degree <= degrees)[:, None])
        columns.append(jnp.where(keep, current, jnp.float32(0.0)))
        following = ((2.0 * degree + 1.0) * coord * current - degree * previous) / (degree + 1.0)
        previous, current = (current, following)
    poly_part = jnp.stack(columns, axis=2)
    bins = jnp.logical_and(
        ground_rows[:, :, None] == jnp.arange(NGB)[None, None, :], inside[:, :, None]
    ).astype(jnp.float32)
    return jnp.concatenate([poly_part, bins], axis=2).astype(jnp.bfloat16)


def per_device(pointing, ground_bin, degrees, lengths, tile_lists, owner_map):
    scan_count, sample_rows, width = pointing.shape
    n_sy = lax.axis_size("sy")
    n_sx = lax.axis_size("sx")
    n_scan = n_sy * n_sx
    n_tile = lax.axis_size("tile")
    sy = lax.axis_index("sy")
    sx = lax.axis_index("sx")
    scan_index = sy * n_sx + sx
    k_tiles = tile_lists.shape[1]
    tile_pixels = width // k_tiles
    col_width = tile_pixels
    half = k_tiles // 2 + 1
    template_cols = DEG_MAX + NGB

    position = scan_index * sample_rows + jnp.arange(sample_rows)
    inside = position[None, :] < lengths[:, None]
    masked = jnp.where(inside[:, :, None], pointing, jnp.zeros_like(pointing))
    template = build_templates(ground_bin, position, lengths, degrees)
    pad = jnp.zeros((scan_count, sample_rows, tile_pixels - template_cols), jnp.bfloat16)
    local = jnp.concatenate([masked, template, pad], axis=2)

    def shifted(x, axis, n, d):
        return lax.ppermute(x, axis, [(i, (i + d) % n) for i in range(n)])

    def column_sums(one, gather_axis, n_gather, reduce_axis, n_reduce, reduce_index):
        rows_all = jnp.concatenate(
            [one] + [shifted(one, gather_axis, n_gather, d) for d in range(1, n_gather)], axis=1
        )
        rows = rows_all[:, :, :width]
        tpl = rows_all[:, :, width : width + template_cols]
        if reduce_axis == "sy":
            firsts = [((reduce_index + d) % n_reduce) * n_sx + sx for d in range(n_reduce)]
        else:
            firsts = [sy * n_sx + (reduce_index + d) % n_reduce for d in range(n_reduce)]
        cols = jnp.concatenate(
            [lax.dynamic_slice_in_dim(rows, f * tile_pixels, tile_pixels, 2) for f in firsts], axis=2
        )
        grams = jnp.einsum("snp,snq->pq", rows, cols, preferred_element_type=jnp.float32)
        projs = jnp.einsum("snt,snp->tp", tpl, rows, preferred_element_type=jnp.float32)
        projs = jnp.swapaxes(projs.reshape(template_cols, k_tiles, tile_pixels), 0, 1)
        projs = projs.reshape(k_tiles * template_cols, tile_pixels)
        norm = jnp.einsum("snt,snu->tu", tpl, tpl, preferred_element_type=jnp.float32)
        norm = jnp.pad(norm, ((0, 0), (0, col_width - template_cols)))
        summed = None
        for d in range(n_reduce):
            part = jnp.concatenate([grams[:, d * col_width : (d + 1) * col_width], projs, norm], axis=0)
            part = part if d == 0 else shifted(part, reduce_axis, n_reduce, d)
            summed = part if summed is None else summed + part
        return summed

    summed = jnp.stack(
        [
            column_sums(local[0:1], "sx", n_sx, "sy", n_sy, sy),
            column_sums(local[1:2], "sy", n_sy, "sx", n_sx, sx),
        ]
    )
    gram = summed[:, :width]
    proj = summed[:, width : width + k_tiles * template_cols].reshape(scan_count, k_tiles, template_cols, tile_pixels)
    proj = jnp.swapaxes(proj, 1, 2).reshape(scan_count, template_cols, width)
    normal = summed[:, width + k_tiles * template_cols :, :template_cols]
    normal = normal + jnp.eye(template_cols, dtype=jnp.float32)[None]
    factor = jnp.linalg.cholesky(normal)
    whitened = jax.scipy.linalg.solve_triangular(factor, proj, lower=True)
    w_col = lax.dynamic_slice_in_dim(whitened, scan_index * tile_pixels, tile_pixels, 2)
    correction = jnp.einsum("stp,stq->spq", whitened, w_col, precision=lax.Precision.HIGHEST)
    contrib = gram - correction

    k_cols = 1
    tile_rows = contrib.reshape(scan_count * k_tiles, tile_pixels, col_width)
    row_tiles = tile_lists.reshape(-1)
    matches = row_tiles[:, None] == jnp.arange(owner_map.shape[0])[None, :]
    owners = jnp.sum(jnp.where(matches, owner_map[None, :], 0), axis=1)
    row_total = scan_count * k_tiles
    capacity = row_total // n_tile
    ordering = jnp.argsort(owners * row_total + jnp.arange(row_total), stable=True)
    local_cols = (
        lax.dynamic_slice_in_dim(tile_lists, scan_index * k_cols, k_cols, 1) - scan_index * n_tile
    )
    local_cols = jnp.repeat(local_cols, k_tiles, axis=0)
    labels = jnp.concatenate([(row_tiles // n_tile)[:, None], local_cols], axis=1)
    send_rows = tile_rows[ordering].reshape(n_tile, capacity, tile_pixels, col_width)
    send_labels = labels[ordering].reshape(n_tile, capacity, 1 + k_cols)
    recv_rows, recv_labels = (
        lax.all_to_all(send_rows, "tile", split_axis=0, concat_axis=0, tiled=True),
        lax.all_to_all(send_labels, "tile", split_axis=0, concat_axis=0, tiled=True),
    )
    item_total = n_tile * capacity
    recv_rows = recv_rows.reshape(item_total, tile_pixels, k_cols, tile_pixels)
    recv_labels = recv_labels.reshape(item_total, 1 + k_cols)
    row_select = (recv_labels[:, 0:1] == jnp.arange(n_scan)[None, :]).astype(jnp.float32)
    col_select = (recv_labels[:, 1:, None] == jnp.arange(n_tile)[None, None, :]).astype(jnp.float32)
    placing = row_select[:, :, None, None] * col_select[:, None, :, :]
    placed = jnp.einsum("irkc,ixky->rxcy", placing, recv_rows, precision=lax.Precision.HIGHEST)
    return placed.reshape(n_scan * tile_pixels, n_tile * tile_pixels)


def solution(mesh):
    devices = mesh.devices.transpose([mesh.axis_names.index("scan"), mesh.axis_names.index("tile")])
    n_scan, n_tile = devices.shape
    n_sx = 4 if n_scan % 4 == 0 else 1
    sub = Mesh(devices.reshape(n_scan // n_sx, n_sx, n_tile), ("sy", "sx", "tile"))
    return jax.shard_map(
        per_device,
        mesh=sub,
        in_specs=(
            P("tile", SCAN_AXES, None),
            P("tile", SCAN_AXES),
            P("tile"),
            P("tile"),
            P("tile", None),
            P(),
        ),
        out_specs=P("tile", SCAN_AXES),
        check_vma=False,
    )
```

```python
import jax
import jax.numpy as jnp
from jax import lax
from jax.experimental import pallas as pl
from jax.experimental.pallas import tpu as pltpu
from jax.sharding import Mesh, PartitionSpec as P

DEG_MAX = 8
NGB = 24
SCAN_AXES = ("sy", "sx")


def build_templates(ground_rows, position, lengths, degrees):
    position = position.astype(jnp.float32)
    length_value = lengths.astype(jnp.float32)[:, None]
    inside = position[None, :] < length_value
    coord = 2.0 * (position[None, :] + 0.5) / length_value - 1.0
    columns = []
    previous = jnp.ones_like(coord)
    current = coord
    for degree in range(1, DEG_MAX + 1):
        keep = jnp.logical_and(inside, (degree <= degrees)[:, None])
        columns.append(jnp.where(keep, current, jnp.float32(0.0)))
        following = ((2.0 * degree + 1.0) * coord * current - degree * previous) / (degree + 1.0)
        previous, current = (current, following)
    poly_part = jnp.stack(columns, axis=2)
    bins = jnp.logical_and(
        ground_rows[:, :, None] == jnp.arange(NGB)[None, None, :], inside[:, :, None]
    ).astype(jnp.float32)
    return jnp.concatenate([poly_part, bins], axis=2).astype(jnp.bfloat16)


def per_device(pointing, ground_bin, degrees, lengths, tile_lists, owner_map):
    scan_count, sample_rows, width = pointing.shape
    n_sy = lax.axis_size("sy")
    n_sx = lax.axis_size("sx")
    n_scan = n_sy * n_sx
    n_tile = lax.axis_size("tile")
    sy = lax.axis_index("sy")
    sx = lax.axis_index("sx")
    scan_index = sy * n_sx + sx
    k_tiles = tile_lists.shape[1]
    tile_pixels = width // k_tiles
    col_width = tile_pixels
    half = k_tiles // 2 + 1
    template_cols = DEG_MAX + NGB

    position = scan_index * sample_rows + jnp.arange(sample_rows)
    inside = position[None, :] < lengths[:, None]
    masked = jnp.where(inside[:, :, None], pointing, jnp.zeros_like(pointing))
    template = build_templates(ground_bin, position, lengths, degrees)
    pad = jnp.zeros((scan_count, sample_rows, tile_pixels - template_cols), jnp.bfloat16)
    local = jnp.concatenate([masked, template, pad], axis=2)

    def shifted(x, axis, n, d):
        return lax.ppermute(x, axis, [(i, (i + d) % n) for i in range(n)])

    def column_sums(one, gather_axis, n_gather, reduce_axis, n_reduce, reduce_index):
        rows_all = jnp.concatenate(
            [one] + [shifted(one, gather_axis, n_gather, d) for d in range(1, n_gather)], axis=1
        )
        rows = rows_all[:, :, :width]
        tpl = rows_all[:, :, width : width + template_cols]
        if reduce_axis == "sy":
            firsts = [((reduce_index + d) % n_reduce) * n_sx + sx for d in range(n_reduce)]
        else:
            firsts = [sy * n_sx + (reduce_index + d) % n_reduce for d in range(n_reduce)]
        cols = jnp.concatenate(
            [lax.dynamic_slice_in_dim(rows, f * tile_pixels, tile_pixels, 2) for f in firsts], axis=2
        )
        grams = jnp.einsum("snp,snq->pq", rows, cols, preferred_element_type=jnp.float32)
        projs = jnp.einsum("snt,snp->tp", tpl, rows, preferred_element_type=jnp.float32)
        projs = jnp.swapaxes(projs.reshape(template_cols, k_tiles, tile_pixels), 0, 1)
        projs = projs.reshape(k_tiles * template_cols, tile_pixels)
        norm = jnp.einsum("snt,snu->tu", tpl, tpl, preferred_element_type=jnp.float32)
        norm = jnp.pad(norm, ((0, 0), (0, col_width - template_cols)))
        summed = None
        for d in range(n_reduce):
            part = jnp.concatenate([grams[:, d * col_width : (d + 1) * col_width], projs, norm], axis=0)
            part = part if d == 0 else shifted(part, reduce_axis, n_reduce, d)
            summed = part if summed is None else summed + part
        return summed

    summed = jnp.stack(
        [
            column_sums(local[0:1], "sx", n_sx, "sy", n_sy, sy),
            column_sums(local[1:2], "sy", n_sy, "sx", n_sx, sx),
        ]
    )
    gram = summed[:, :width]
    proj = summed[:, width : width + k_tiles * template_cols].reshape(scan_count, k_tiles, template_cols, tile_pixels)
    proj = jnp.swapaxes(proj, 1, 2).reshape(scan_count, template_cols, width)
    normal = summed[:, width + k_tiles * template_cols :, :template_cols]
    normal = normal + jnp.eye(template_cols, dtype=jnp.float32)[None]
    factor = jnp.linalg.cholesky(normal)
    whitened = jax.scipy.linalg.solve_triangular(factor, proj, lower=True)
    w_col = lax.dynamic_slice_in_dim(whitened, scan_index * tile_pixels, tile_pixels, 2)
    correction = jnp.einsum("stp,stq->spq", whitened, w_col, precision=lax.Precision.HIGHEST)
    contrib = gram - correction

    k_cols = 1
    tile_rows = contrib.reshape(scan_count * k_tiles, tile_pixels, col_width)
    row_tiles = tile_lists.reshape(-1)
    matches = row_tiles[:, None] == jnp.arange(owner_map.shape[0])[None, :]
    owners = jnp.sum(jnp.where(matches, owner_map[None, :], 0), axis=1)
    row_total = scan_count * k_tiles
    capacity = row_total // n_tile
    ordering = jnp.argsort(owners * row_total + jnp.arange(row_total), stable=True)
    local_cols = (
        lax.dynamic_slice_in_dim(tile_lists, scan_index * k_cols, k_cols, 1) - scan_index * n_tile
    )
    local_cols = jnp.repeat(local_cols, k_tiles, axis=0)
    labels = jnp.concatenate([(row_tiles // n_tile)[:, None], local_cols], axis=1)
    send_rows = tile_rows[ordering].reshape(n_tile, capacity, tile_pixels, col_width)
    send_labels = labels[ordering].reshape(n_tile, capacity, 1 + k_cols)
    recv_rows, recv_labels = (
        lax.all_to_all(send_rows, "tile", split_axis=0, concat_axis=0, tiled=True),
        lax.all_to_all(send_labels, "tile", split_axis=0, concat_axis=0, tiled=True),
    )
    item_total = n_tile * capacity
    recv_rows = recv_rows.reshape(item_total, tile_pixels, tile_pixels)
    recv_labels = recv_labels.reshape(item_total, 1 + k_cols)
    return place(recv_rows, recv_labels[:, 0], recv_labels[:, 1], n_scan, n_tile)


def place(recv, row_block, col_block, n_rows, n_cols):
    items, tile_pixels, _ = recv.shape

    def kernel(row_ref, col_ref, recv_ref, out_ref):
        r = pl.program_id(0)
        out_ref[...] = jnp.zeros(out_ref.shape, out_ref.dtype)

        def body(i, carry):
            for c in range(n_cols):
                @pl.when(jnp.logical_and(row_ref[i] == r, col_ref[i] == c))
                def _():
                    out_ref[:, c * tile_pixels : (c + 1) * tile_pixels] += recv_ref[i]

            return carry

        lax.fori_loop(0, items, body, 0)

    return pl.pallas_call(
        kernel,
        grid_spec=pltpu.PrefetchScalarGridSpec(
            num_scalar_prefetch=2,
            grid=(n_rows,),
            in_specs=[pl.BlockSpec((items, tile_pixels, tile_pixels), lambda r, a, b: (0, 0, 0))],
            out_specs=pl.BlockSpec((tile_pixels, n_cols * tile_pixels), lambda r, a, b: (r, 0)),
        ),
        out_shape=jax.ShapeDtypeStruct((n_rows * tile_pixels, n_cols * tile_pixels), jnp.float32),
    )(row_block, col_block, recv)


def solution(mesh):
    devices = mesh.devices.transpose([mesh.axis_names.index("scan"), mesh.axis_names.index("tile")])
    n_scan, n_tile = devices.shape
    n_sx = 4 if n_scan % 4 == 0 else 1
    sub = Mesh(devices.reshape(n_scan // n_sx, n_sx, n_tile), ("sy", "sx", "tile"))
    return jax.shard_map(
        per_device,
        mesh=sub,
        in_specs=(
            P("tile", SCAN_AXES, None),
            P("tile", SCAN_AXES),
            P("tile"),
            P("tile"),
            P("tile", None),
            P(),
        ),
        out_specs=P("tile", SCAN_AXES),
        check_vma=False,
    )
```

```python
import jax
import jax.numpy as jnp
from jax import lax
from jax.experimental import pallas as pl
from jax.experimental.pallas import tpu as pltpu
from jax.sharding import Mesh, PartitionSpec as P

DEG_MAX = 8
NGB = 24
SCAN_AXES = ("sy", "sx")


def build_templates(ground_rows, position, lengths, degrees):
    position = position.astype(jnp.float32)
    length_value = lengths.astype(jnp.float32)[:, None]
    inside = position[None, :] < length_value
    coord = 2.0 * (position[None, :] + 0.5) / length_value - 1.0
    columns = []
    previous = jnp.ones_like(coord)
    current = coord
    for degree in range(1, DEG_MAX + 1):
        keep = jnp.logical_and(inside, (degree <= degrees)[:, None])
        columns.append(jnp.where(keep, current, jnp.float32(0.0)))
        following = ((2.0 * degree + 1.0) * coord * current - degree * previous) / (degree + 1.0)
        previous, current = (current, following)
    poly_part = jnp.stack(columns, axis=2)
    bins = jnp.logical_and(
        ground_rows[:, :, None] == jnp.arange(NGB)[None, None, :], inside[:, :, None]
    ).astype(jnp.float32)
    return jnp.concatenate([poly_part, bins], axis=2).astype(jnp.bfloat16)


def per_device(pointing, ground_bin, degrees, lengths, tile_lists, owner_map):
    scan_count, sample_rows, width = pointing.shape
    n_sy = lax.axis_size("sy")
    n_sx = lax.axis_size("sx")
    n_scan = n_sy * n_sx
    n_tile = lax.axis_size("tile")
    sy = lax.axis_index("sy")
    sx = lax.axis_index("sx")
    scan_index = sy * n_sx + sx
    k_tiles = tile_lists.shape[1]
    tile_pixels = width // k_tiles
    col_width = tile_pixels
    half = k_tiles // 2 + 1
    template_cols = DEG_MAX + NGB

    position = scan_index * sample_rows + jnp.arange(sample_rows)
    inside = position[None, :] < lengths[:, None]
    masked = jnp.where(inside[:, :, None], pointing, jnp.zeros_like(pointing))
    template = build_templates(ground_bin, position, lengths, degrees)
    pad = jnp.zeros((scan_count, sample_rows, tile_pixels - template_cols), jnp.bfloat16)
    local = jnp.concatenate([masked, template, pad], axis=2)

    def shifted(x, axis, n, d):
        return lax.ppermute(x, axis, [(i, (i + d) % n) for i in range(n)])

    def column_sums(one, gather_axis, n_gather, reduce_axis, n_reduce, reduce_index):
        rows_all = jnp.concatenate(
            [one] + [shifted(one, gather_axis, n_gather, d) for d in range(1, n_gather)], axis=1
        )
        rows = rows_all[:, :, :width]
        tpl = rows_all[:, :, width : width + template_cols]
        if reduce_axis == "sy":
            firsts = [((reduce_index + d) % n_reduce) * n_sx + sx for d in range(n_reduce)]
        else:
            firsts = [sy * n_sx + (reduce_index + d) % n_reduce for d in range(n_reduce)]
        cols = jnp.concatenate(
            [lax.dynamic_slice_in_dim(rows, f * tile_pixels, tile_pixels, 2) for f in firsts], axis=2
        )
        grams = jnp.einsum("snp,snq->pq", rows, cols, preferred_element_type=jnp.float32)
        projs = jnp.einsum("snt,snp->tp", tpl, rows, preferred_element_type=jnp.float32)
        projs = jnp.swapaxes(projs.reshape(template_cols, k_tiles, tile_pixels), 0, 1)
        projs = projs.reshape(k_tiles * template_cols, tile_pixels)
        norm = jnp.einsum("snt,snu->tu", tpl, tpl, preferred_element_type=jnp.float32)
        norm = jnp.pad(norm, ((0, 0), (0, col_width - template_cols)))
        summed = None
        for d in range(n_reduce):
            part = jnp.concatenate([grams[:, d * col_width : (d + 1) * col_width], projs, norm], axis=0)
            part = part if d == 0 else shifted(part, reduce_axis, n_reduce, d)
            summed = part if summed is None else summed + part
        return summed

    summed = jnp.stack(
        [
            column_sums(local[0:1], "sx", n_sx, "sy", n_sy, sy),
            column_sums(local[1:2], "sy", n_sy, "sx", n_sx, sx),
        ]
    )
    gram = summed[:, :width]
    proj = summed[:, width : width + k_tiles * template_cols].reshape(scan_count, k_tiles, template_cols, tile_pixels)
    proj = jnp.swapaxes(proj, 1, 2).reshape(scan_count, template_cols, width)
    normal = summed[:, width + k_tiles * template_cols :, :template_cols]
    normal = normal + jnp.eye(template_cols, dtype=jnp.float32)[None]
    factor = jnp.linalg.cholesky(normal)
    whitened = jax.scipy.linalg.solve_triangular(factor, proj, lower=True)
    w_col = lax.dynamic_slice_in_dim(whitened, scan_index * tile_pixels, tile_pixels, 2)
    correction = jnp.einsum("stp,stq->spq", whitened, w_col, precision=lax.Precision.HIGHEST)
    contrib = gram - correction

    k_cols = 1
    tile_rows = contrib.reshape(scan_count * k_tiles, tile_pixels, col_width)
    row_tiles = tile_lists.reshape(-1)
    matches = row_tiles[:, None] == jnp.arange(owner_map.shape[0])[None, :]
    owners = jnp.sum(jnp.where(matches, owner_map[None, :], 0), axis=1)
    row_total = scan_count * k_tiles
    capacity = row_total // n_tile
    ordering = jnp.argsort(owners * row_total + jnp.arange(row_total), stable=True)
    local_cols = (
        lax.dynamic_slice_in_dim(tile_lists, scan_index * k_cols, k_cols, 1) - scan_index * n_tile
    )
    local_cols = jnp.repeat(local_cols, k_tiles, axis=0)
    labels = jnp.concatenate([(row_tiles // n_tile)[:, None], local_cols], axis=1)
    send_rows = tile_rows[ordering].reshape(n_tile, capacity, tile_pixels, col_width)
    send_labels = labels[ordering].reshape(n_tile, capacity, 1 + k_cols)
    recv_rows, recv_labels = (
        lax.all_to_all(send_rows, "tile", split_axis=0, concat_axis=0, tiled=True),
        lax.all_to_all(send_labels, "tile", split_axis=0, concat_axis=0, tiled=True),
    )
    item_total = n_tile * capacity
    recv_rows = recv_rows.reshape(item_total, tile_pixels, tile_pixels)
    recv_labels = recv_labels.reshape(item_total, 1 + k_cols)
    return place(recv_rows, recv_labels[:, 0], recv_labels[:, 1], n_scan, n_tile)


def place(recv, row_block, col_block, n_rows, n_cols):
    items, tile_pixels, _ = recv.shape

    def kernel(row_ref, col_ref, recv_ref, out_ref):
        r = pl.program_id(0)
        out_ref[...] = jnp.zeros(out_ref.shape, out_ref.dtype)

        for i in range(items):
            @pl.when(row_ref[i] == r)
            def _():
                at = pl.ds(pl.multiple_of(col_ref[i] * tile_pixels, tile_pixels), tile_pixels)
                out_ref[:, at] += recv_ref[i]

    return pl.pallas_call(
        kernel,
        grid_spec=pltpu.PrefetchScalarGridSpec(
            num_scalar_prefetch=2,
            grid=(n_rows,),
            in_specs=[pl.BlockSpec((items, tile_pixels, tile_pixels), lambda r, a, b: (0, 0, 0))],
            out_specs=pl.BlockSpec((tile_pixels, n_cols * tile_pixels), lambda r, a, b: (r, 0)),
        ),
        out_shape=jax.ShapeDtypeStruct((n_rows * tile_pixels, n_cols * tile_pixels), jnp.float32),
    )(row_block, col_block, recv)


def solution(mesh):
    devices = mesh.devices.transpose([mesh.axis_names.index("scan"), mesh.axis_names.index("tile")])
    n_scan, n_tile = devices.shape
    n_sx = 4 if n_scan % 4 == 0 else 1
    sub = Mesh(devices.reshape(n_scan // n_sx, n_sx, n_tile), ("sy", "sx", "tile"))
    return jax.shard_map(
        per_device,
        mesh=sub,
        in_specs=(
            P("tile", SCAN_AXES, None),
            P("tile", SCAN_AXES),
            P("tile"),
            P("tile"),
            P("tile", None),
            P(),
        ),
        out_specs=P("tile", SCAN_AXES),
        check_vma=False,
    )
```

```python
import jax
import jax.numpy as jnp
from jax import lax
from jax.experimental import pallas as pl
from jax.experimental.pallas import tpu as pltpu
from jax.sharding import Mesh, PartitionSpec as P

DEG_MAX = 8
NGB = 24
SCAN_AXES = ("sy", "sx")


def build_templates(ground_rows, position, lengths, degrees):
    position = position.astype(jnp.float32)
    length_value = lengths.astype(jnp.float32)[:, None]
    inside = position[None, :] < length_value
    coord = 2.0 * (position[None, :] + 0.5) / length_value - 1.0
    columns = []
    previous = jnp.ones_like(coord)
    current = coord
    for degree in range(1, DEG_MAX + 1):
        keep = jnp.logical_and(inside, (degree <= degrees)[:, None])
        columns.append(jnp.where(keep, current, jnp.float32(0.0)))
        following = ((2.0 * degree + 1.0) * coord * current - degree * previous) / (degree + 1.0)
        previous, current = (current, following)
    poly_part = jnp.stack(columns, axis=2)
    bins = jnp.logical_and(
        ground_rows[:, :, None] == jnp.arange(NGB)[None, None, :], inside[:, :, None]
    ).astype(jnp.float32)
    return jnp.concatenate([poly_part, bins], axis=2).astype(jnp.bfloat16)


def per_device(pointing, ground_bin, degrees, lengths, tile_lists, owner_map):
    scan_count, sample_rows, width = pointing.shape
    n_sy = lax.axis_size("sy")
    n_sx = lax.axis_size("sx")
    n_scan = n_sy * n_sx
    n_tile = lax.axis_size("tile")
    sy = lax.axis_index("sy")
    sx = lax.axis_index("sx")
    scan_index = sy * n_sx + sx
    k_tiles = tile_lists.shape[1]
    tile_pixels = width // k_tiles
    col_width = tile_pixels
    half = k_tiles // 2 + 1
    template_cols = DEG_MAX + NGB

    position = scan_index * sample_rows + jnp.arange(sample_rows)
    inside = position[None, :] < lengths[:, None]
    masked = jnp.where(inside[:, :, None], pointing, jnp.zeros_like(pointing))
    template = build_templates(ground_bin, position, lengths, degrees)
    pad = jnp.zeros((scan_count, sample_rows, tile_pixels - template_cols), jnp.bfloat16)
    local = jnp.concatenate([masked, template, pad], axis=2)

    bins_all = lax.all_gather(ground_bin.astype(jnp.bfloat16), SCAN_AXES, axis=1, tiled=True)
    template_all = build_templates(
        bins_all.astype(jnp.int32), jnp.arange(n_scan * sample_rows), lengths, degrees
    )
    normal = jnp.einsum("snt,snu->stu", template_all, template_all, preferred_element_type=jnp.float32)
    normal = normal + jnp.eye(template_cols, dtype=jnp.float32)[None]
    factor = jnp.linalg.cholesky(normal)
    eye = jnp.broadcast_to(jnp.eye(template_cols, dtype=jnp.float32), normal.shape)
    inverse = jax.scipy.linalg.solve_triangular(factor, eye, lower=True)

    def shifted(x, axis, n, d):
        return lax.ppermute(x, axis, [(i, (i + d) % n) for i in range(n)])

    def column_sums(one, gather_axis, n_gather, reduce_axis, n_reduce, reduce_index):
        rows_all = jnp.concatenate(
            [one] + [shifted(one, gather_axis, n_gather, d) for d in range(1, n_gather)], axis=1
        )
        rows = rows_all[:, :, :width]
        tpl = rows_all[:, :, width : width + template_cols]
        if reduce_axis == "sy":
            firsts = [((reduce_index + d) % n_reduce) * n_sx + sx for d in range(n_reduce)]
        else:
            firsts = [sy * n_sx + (reduce_index + d) % n_reduce for d in range(n_reduce)]
        cols = jnp.concatenate(
            [lax.dynamic_slice_in_dim(rows, f * tile_pixels, tile_pixels, 2) for f in firsts], axis=2
        )
        grams = jnp.einsum("snp,snq->pq", rows, cols, preferred_element_type=jnp.float32)
        projs = jnp.einsum("snt,snp->tp", tpl, rows, preferred_element_type=jnp.float32)
        projs = jnp.swapaxes(projs.reshape(template_cols, k_tiles, tile_pixels), 0, 1)
        projs = projs.reshape(k_tiles * template_cols, tile_pixels)
        summed = None
        for d in range(n_reduce):
            part = jnp.concatenate([grams[:, d * col_width : (d + 1) * col_width], projs], axis=0)
            part = part if d == 0 else shifted(part, reduce_axis, n_reduce, d)
            summed = part if summed is None else summed + part
        return summed

    summed = jnp.stack(
        [
            column_sums(local[0:1], "sx", n_sx, "sy", n_sy, sy),
            column_sums(local[1:2], "sy", n_sy, "sx", n_sx, sx),
        ]
    )
    gram = summed[:, :width]
    proj = summed[:, width : width + k_tiles * template_cols].reshape(scan_count, k_tiles, template_cols, tile_pixels)
    proj = jnp.swapaxes(proj, 1, 2).reshape(scan_count, template_cols, width)
    whitened = jnp.einsum("stu,sup->stp", inverse, proj, precision=lax.Precision.HIGHEST)
    w_col = lax.dynamic_slice_in_dim(whitened, scan_index * tile_pixels, tile_pixels, 2)
    correction = jnp.einsum("stp,stq->spq", whitened, w_col, precision=lax.Precision.HIGHEST)
    contrib = gram - correction

    k_cols = 1
    tile_rows = contrib.reshape(scan_count * k_tiles, tile_pixels, col_width)
    row_tiles = tile_lists.reshape(-1)
    matches = row_tiles[:, None] == jnp.arange(owner_map.shape[0])[None, :]
    owners = jnp.sum(jnp.where(matches, owner_map[None, :], 0), axis=1)
    row_total = scan_count * k_tiles
    capacity = row_total // n_tile
    ordering = jnp.argsort(owners * row_total + jnp.arange(row_total), stable=True)
    local_cols = (
        lax.dynamic_slice_in_dim(tile_lists, scan_index * k_cols, k_cols, 1) - scan_index * n_tile
    )
    local_cols = jnp.repeat(local_cols, k_tiles, axis=0)
    labels = jnp.concatenate([(row_tiles // n_tile)[:, None], local_cols], axis=1)
    send_rows = tile_rows[ordering].reshape(n_tile, capacity, tile_pixels, col_width)
    send_labels = labels[ordering].reshape(n_tile, capacity, 1 + k_cols)
    recv_rows, recv_labels = (
        lax.all_to_all(send_rows, "tile", split_axis=0, concat_axis=0, tiled=True),
        lax.all_to_all(send_labels, "tile", split_axis=0, concat_axis=0, tiled=True),
    )
    item_total = n_tile * capacity
    recv_rows = recv_rows.reshape(item_total, tile_pixels, tile_pixels)
    recv_labels = recv_labels.reshape(item_total, 1 + k_cols)
    return place(recv_rows, recv_labels[:, 0], recv_labels[:, 1], n_scan, n_tile)


def place(recv, row_block, col_block, n_rows, n_cols):
    items, tile_pixels, _ = recv.shape

    def kernel(row_ref, col_ref, recv_ref, out_ref):
        r = pl.program_id(0)
        out_ref[...] = jnp.zeros(out_ref.shape, out_ref.dtype)

        for i in range(items):
            @pl.when(row_ref[i] == r)
            def _():
                at = pl.ds(pl.multiple_of(col_ref[i] * tile_pixels, tile_pixels), tile_pixels)
                out_ref[:, at] += recv_ref[i]

    return pl.pallas_call(
        kernel,
        grid_spec=pltpu.PrefetchScalarGridSpec(
            num_scalar_prefetch=2,
            grid=(n_rows,),
            in_specs=[pl.BlockSpec((items, tile_pixels, tile_pixels), lambda r, a, b: (0, 0, 0))],
            out_specs=pl.BlockSpec((tile_pixels, n_cols * tile_pixels), lambda r, a, b: (r, 0)),
        ),
        out_shape=jax.ShapeDtypeStruct((n_rows * tile_pixels, n_cols * tile_pixels), jnp.float32),
    )(row_block, col_block, recv)


def solution(mesh):
    devices = mesh.devices.transpose([mesh.axis_names.index("scan"), mesh.axis_names.index("tile")])
    n_scan, n_tile = devices.shape
    n_sx = 4 if n_scan % 4 == 0 else 1
    sub = Mesh(devices.reshape(n_scan // n_sx, n_sx, n_tile), ("sy", "sx", "tile"))
    return jax.shard_map(
        per_device,
        mesh=sub,
        in_specs=(
            P("tile", SCAN_AXES, None),
            P("tile", SCAN_AXES),
            P("tile"),
            P("tile"),
            P("tile", None),
            P(),
        ),
        out_specs=P("tile", SCAN_AXES),
        check_vma=False,
    )
```

```python
import jax
import jax.numpy as jnp
from jax import lax
from jax.experimental import pallas as pl
from jax.experimental.pallas import tpu as pltpu
from jax.sharding import Mesh, PartitionSpec as P

DEG_MAX = 8
NGB = 24
SCAN_AXES = ("sy", "sx")


def build_templates(ground_rows, position, lengths, degrees):
    position = position.astype(jnp.float32)
    length_value = lengths.astype(jnp.float32)[:, None]
    inside = position[None, :] < length_value
    coord = 2.0 * (position[None, :] + 0.5) / length_value - 1.0
    columns = []
    previous = jnp.ones_like(coord)
    current = coord
    for degree in range(1, DEG_MAX + 1):
        keep = jnp.logical_and(inside, (degree <= degrees)[:, None])
        columns.append(jnp.where(keep, current, jnp.float32(0.0)))
        following = ((2.0 * degree + 1.0) * coord * current - degree * previous) / (degree + 1.0)
        previous, current = (current, following)
    poly_part = jnp.stack(columns, axis=2)
    bins = jnp.logical_and(
        ground_rows[:, :, None] == jnp.arange(NGB)[None, None, :], inside[:, :, None]
    ).astype(jnp.float32)
    return jnp.concatenate([poly_part, bins], axis=2).astype(jnp.bfloat16)


def per_device(pointing, ground_bin, degrees, lengths, tile_lists, owner_map):
    scan_count, sample_rows, width = pointing.shape
    n_sy = lax.axis_size("sy")
    n_sx = lax.axis_size("sx")
    n_scan = n_sy * n_sx
    n_tile = lax.axis_size("tile")
    sy = lax.axis_index("sy")
    sx = lax.axis_index("sx")
    scan_index = sy * n_sx + sx
    k_tiles = tile_lists.shape[1]
    tile_pixels = width // k_tiles
    col_width = tile_pixels
    half = k_tiles // 2 + 1
    template_cols = DEG_MAX + NGB

    position = scan_index * sample_rows + jnp.arange(sample_rows)
    inside = position[None, :] < lengths[:, None]
    masked = jnp.where(inside[:, :, None], pointing, jnp.zeros_like(pointing))
    template = build_templates(ground_bin, position, lengths, degrees)
    pad = jnp.zeros((scan_count, sample_rows, tile_pixels - template_cols), jnp.bfloat16)
    local = jnp.concatenate([masked, template, pad], axis=2)

    bins_all = lax.all_gather(ground_bin.astype(jnp.bfloat16), SCAN_AXES, axis=1, tiled=True)
    template_all = build_templates(
        bins_all.astype(jnp.int32), jnp.arange(n_scan * sample_rows), lengths, degrees
    )
    normal = jnp.einsum("snt,snu->stu", template_all, template_all, preferred_element_type=jnp.float32)
    normal = normal + jnp.eye(template_cols, dtype=jnp.float32)[None]
    factor = jnp.linalg.cholesky(normal)
    eye = jnp.broadcast_to(jnp.eye(template_cols, dtype=jnp.float32), normal.shape)
    inverse = jax.scipy.linalg.solve_triangular(factor, eye, lower=True)

    def shifted(x, axis, n, d):
        return lax.ppermute(x, axis, [(i, (i + d) % n) for i in range(n)])

    def column_sums(one, gather_axis, n_gather, reduce_axis, n_reduce, reduce_index):
        rows_all = jnp.concatenate(
            [one] + [shifted(one, gather_axis, n_gather, d) for d in range(1, n_gather)], axis=1
        )
        rows = rows_all[:, :, :width]
        tpl = rows_all[:, :, width : width + template_cols]
        if reduce_axis == "sy":
            firsts = [((reduce_index + d) % n_reduce) * n_sx + sx for d in range(n_reduce)]
        else:
            firsts = [sy * n_sx + (reduce_index + d) % n_reduce for d in range(n_reduce)]
        cols = jnp.concatenate(
            [lax.dynamic_slice_in_dim(rows, f * tile_pixels, tile_pixels, 2) for f in firsts], axis=2
        )
        grams = jnp.einsum("snp,snq->pq", rows, cols, preferred_element_type=jnp.float32)
        projs = jnp.einsum("snt,snp->tp", tpl, rows, preferred_element_type=jnp.float32)
        projs = jnp.swapaxes(projs.reshape(template_cols, k_tiles, tile_pixels), 0, 1)
        projs = projs.reshape(k_tiles * template_cols, tile_pixels)
        summed = None
        for d in range(n_reduce):
            part = jnp.concatenate([grams[:, d * col_width : (d + 1) * col_width], projs], axis=0)
            part = part if d == 0 else shifted(part, reduce_axis, n_reduce, d)
            summed = part if summed is None else summed + part
        return summed

    summed = jnp.stack(
        [
            column_sums(local[0:1], "sx", n_sx, "sy", n_sy, sy),
            column_sums(local[1:2], "sy", n_sy, "sx", n_sx, sx),
        ]
    )
    gram = summed[:, :width]
    proj = summed[:, width : width + k_tiles * template_cols].reshape(scan_count, k_tiles, template_cols, tile_pixels)
    proj = jnp.swapaxes(proj, 1, 2).reshape(scan_count, template_cols, width)
    whitened = jnp.einsum("stu,sup->stp", inverse, proj, precision=lax.Precision.HIGHEST)
    w_col = lax.dynamic_slice_in_dim(whitened, scan_index * tile_pixels, tile_pixels, 2)
    correction = jnp.einsum("stp,stq->spq", whitened, w_col, precision=lax.Precision.HIGHEST)
    contrib = gram - correction

    k_cols = 1
    tile_rows = contrib.reshape(scan_count * k_tiles, tile_pixels, col_width)
    row_tiles = tile_lists.reshape(-1)
    matches = row_tiles[:, None] == jnp.arange(owner_map.shape[0])[None, :]
    owners = jnp.sum(jnp.where(matches, owner_map[None, :], 0), axis=1)
    row_total = scan_count * k_tiles
    capacity = row_total // n_tile
    ordering = jnp.argsort(owners * row_total + jnp.arange(row_total), stable=True)
    local_cols = (
        lax.dynamic_slice_in_dim(tile_lists, scan_index * k_cols, k_cols, 1) - scan_index * n_tile
    )
    local_cols = jnp.repeat(local_cols, k_tiles, axis=0)
    labels = jnp.concatenate([(row_tiles // n_tile)[:, None], local_cols], axis=1)
    send_rows = tile_rows[ordering].reshape(n_tile, capacity, tile_pixels, col_width)
    send_labels = labels[ordering].reshape(n_tile, capacity, 1 + k_cols)
    recv_rows, recv_labels = (
        lax.all_to_all(send_rows, "tile", split_axis=0, concat_axis=0, tiled=True),
        lax.all_to_all(send_labels, "tile", split_axis=0, concat_axis=0, tiled=True),
    )
    item_total = n_tile * capacity
    recv_rows = recv_rows.reshape(item_total, tile_pixels, tile_pixels)
    recv_labels = recv_labels.reshape(item_total, 1 + k_cols)
    row_block = recv_labels[:, 0]
    order = jnp.argsort(row_block).astype(jnp.int32)
    counts = jnp.sum(row_block[:, None] == jnp.arange(n_scan)[None, :], axis=0)
    starts = jnp.concatenate([jnp.zeros((1,), jnp.int32), jnp.cumsum(counts).astype(jnp.int32)])
    return place(recv_rows, order, starts, recv_labels[:, 1], n_scan, n_tile)


def place(recv, order, starts, col_block, n_rows, n_cols):
    items, tile_pixels, _ = recv.shape

    def kernel(order_ref, starts_ref, col_ref, recv_ref, out_ref):
        r = pl.program_id(0)
        out_ref[...] = jnp.zeros(out_ref.shape, out_ref.dtype)

        def body(k, carry):
            i = order_ref[k]
            at = pl.ds(pl.multiple_of(col_ref[i] * tile_pixels, tile_pixels), tile_pixels)
            out_ref[:, at] += recv_ref[i]
            return carry

        lax.fori_loop(starts_ref[r], starts_ref[r + 1], body, 0)

    return pl.pallas_call(
        kernel,
        grid_spec=pltpu.PrefetchScalarGridSpec(
            num_scalar_prefetch=3,
            grid=(n_rows,),
            in_specs=[pl.BlockSpec((items, tile_pixels, tile_pixels), lambda r, a, b, c: (0, 0, 0))],
            out_specs=pl.BlockSpec((tile_pixels, n_cols * tile_pixels), lambda r, a, b, c: (r, 0)),
        ),
        out_shape=jax.ShapeDtypeStruct((n_rows * tile_pixels, n_cols * tile_pixels), jnp.float32),
    )(order, starts, col_block, recv)


def solution(mesh):
    devices = mesh.devices.transpose([mesh.axis_names.index("scan"), mesh.axis_names.index("tile")])
    n_scan, n_tile = devices.shape
    n_sx = 4 if n_scan % 4 == 0 else 1
    sub = Mesh(devices.reshape(n_scan // n_sx, n_sx, n_tile), ("sy", "sx", "tile"))
    return jax.shard_map(
        per_device,
        mesh=sub,
        in_specs=(
            P("tile", SCAN_AXES, None),
            P("tile", SCAN_AXES),
            P("tile"),
            P("tile"),
            P("tile", None),
            P(),
        ),
        out_specs=P("tile", SCAN_AXES),
        check_vma=False,
    )
```

```python
import jax
import jax.numpy as jnp
from jax import lax
from jax.experimental import pallas as pl
from jax.experimental.pallas import tpu as pltpu
from jax.sharding import Mesh, PartitionSpec as P

DEG_MAX = 8
NGB = 24
SCAN_AXES = ("sy", "sx")


def build_templates(ground_rows, position, lengths, degrees):
    position = position.astype(jnp.float32)
    length_value = lengths.astype(jnp.float32)[:, None]
    inside = position[None, :] < length_value
    coord = 2.0 * (position[None, :] + 0.5) / length_value - 1.0
    columns = []
    previous = jnp.ones_like(coord)
    current = coord
    for degree in range(1, DEG_MAX + 1):
        keep = jnp.logical_and(inside, (degree <= degrees)[:, None])
        columns.append(jnp.where(keep, current, jnp.float32(0.0)))
        following = ((2.0 * degree + 1.0) * coord * current - degree * previous) / (degree + 1.0)
        previous, current = (current, following)
    poly_part = jnp.stack(columns, axis=2)
    bins = jnp.logical_and(
        ground_rows[:, :, None] == jnp.arange(NGB)[None, None, :], inside[:, :, None]
    ).astype(jnp.float32)
    return jnp.concatenate([poly_part, bins], axis=2).astype(jnp.bfloat16)


def per_device(pointing, ground_bin, degrees, lengths, tile_lists, owner_map):
    scan_count, sample_rows, width = pointing.shape
    n_sy = lax.axis_size("sy")
    n_sx = lax.axis_size("sx")
    n_scan = n_sy * n_sx
    n_tile = lax.axis_size("tile")
    sy = lax.axis_index("sy")
    sx = lax.axis_index("sx")
    scan_index = sy * n_sx + sx
    k_tiles = tile_lists.shape[1]
    tile_pixels = width // k_tiles
    col_width = tile_pixels
    half = k_tiles // 2 + 1
    template_cols = DEG_MAX + NGB

    position = scan_index * sample_rows + jnp.arange(sample_rows)
    inside = position[None, :] < lengths[:, None]
    masked = jnp.where(inside[:, :, None], pointing, jnp.zeros_like(pointing))
    template = build_templates(ground_bin, position, lengths, degrees)
    pad = jnp.zeros((scan_count, sample_rows, tile_pixels - template_cols), jnp.bfloat16)
    local = jnp.concatenate([masked, template, pad], axis=2)

    bins_all = lax.all_gather(ground_bin.astype(jnp.bfloat16), SCAN_AXES, axis=1, tiled=True)
    template_all = build_templates(
        bins_all.astype(jnp.int32), jnp.arange(n_scan * sample_rows), lengths, degrees
    )
    normal = jnp.einsum("snt,snu->stu", template_all, template_all, preferred_element_type=jnp.float32)
    normal = normal + jnp.eye(template_cols, dtype=jnp.float32)[None]
    factor = jnp.linalg.cholesky(normal)
    eye = jnp.broadcast_to(jnp.eye(template_cols, dtype=jnp.float32), normal.shape)
    inverse = jax.scipy.linalg.solve_triangular(factor, eye, lower=True)

    def shifted(x, axis, n, d):
        return lax.ppermute(x, axis, [(i, (i + d) % n) for i in range(n)])

    def column_sums(one, gather_axis, n_gather, reduce_axis, n_reduce, reduce_index):
        rows_all = jnp.concatenate(
            [one] + [shifted(one, gather_axis, n_gather, d) for d in range(1, n_gather)], axis=1
        )
        rows = rows_all[:, :, :width]
        tpl = rows_all[:, :, width : width + template_cols]
        if reduce_axis == "sy":
            firsts = [((reduce_index + d) % n_reduce) * n_sx + sx for d in range(n_reduce)]
        else:
            firsts = [sy * n_sx + (reduce_index + d) % n_reduce for d in range(n_reduce)]
        cols = jnp.concatenate(
            [lax.dynamic_slice_in_dim(rows, f * tile_pixels, tile_pixels, 2) for f in firsts], axis=2
        )
        grams = jnp.einsum("snp,snq->pq", rows, cols, preferred_element_type=jnp.float32)
        projs = jnp.einsum("snt,snp->tp", tpl, rows, preferred_element_type=jnp.float32)
        projs = jnp.swapaxes(projs.reshape(template_cols, k_tiles, tile_pixels), 0, 1)
        projs = projs.reshape(k_tiles * template_cols, tile_pixels)
        summed = None
        for d in range(n_reduce):
            part = jnp.concatenate([grams[:, d * col_width : (d + 1) * col_width], projs], axis=0)
            part = part if d == 0 else shifted(part, reduce_axis, n_reduce, d)
            summed = part if summed is None else summed + part
        return summed

    summed = jnp.stack(
        [
            column_sums(local[0:1], "sx", n_sx, "sy", n_sy, sy),
            column_sums(local[1:2], "sy", n_sy, "sx", n_sx, sx),
        ]
    )
    gram = summed[:, :width]
    proj = summed[:, width : width + k_tiles * template_cols].reshape(scan_count, k_tiles, template_cols, tile_pixels)
    proj = jnp.swapaxes(proj, 1, 2).reshape(scan_count, template_cols, width)
    whitened = jnp.einsum("stu,sup->stp", inverse, proj, precision=lax.Precision.HIGHEST)
    w_col = lax.dynamic_slice_in_dim(whitened, scan_index * tile_pixels, tile_pixels, 2)
    correction = jnp.einsum("stp,stq->spq", whitened, w_col, precision=lax.Precision.HIGHEST)
    contrib = gram - correction

    k_cols = 1
    tile_rows = contrib.reshape(scan_count * k_tiles, tile_pixels, col_width)
    row_tiles = tile_lists.reshape(-1)
    matches = row_tiles[:, None] == jnp.arange(owner_map.shape[0])[None, :]
    owners = jnp.sum(jnp.where(matches, owner_map[None, :], 0), axis=1)
    row_total = scan_count * k_tiles
    capacity = row_total // n_tile
    ordering = jnp.argsort(owners * row_total + jnp.arange(row_total), stable=True)
    local_cols = (
        lax.dynamic_slice_in_dim(tile_lists, scan_index * k_cols, k_cols, 1) - scan_index * n_tile
    )
    local_cols = jnp.repeat(local_cols, k_tiles, axis=0)
    labels = jnp.concatenate([(row_tiles // n_tile)[:, None], local_cols], axis=1)
    send_rows = tile_rows[ordering].reshape(n_tile, capacity, tile_pixels, col_width)
    send_labels = labels[ordering].reshape(n_tile, capacity, 1 + k_cols)
    recv_rows, recv_labels = (
        lax.all_to_all(send_rows, "tile", split_axis=0, concat_axis=0, tiled=True),
        lax.all_to_all(send_labels, "tile", split_axis=0, concat_axis=0, tiled=True),
    )
    item_total = n_tile * capacity
    recv_rows = recv_rows.reshape(item_total, tile_pixels, tile_pixels)
    recv_labels = recv_labels.reshape(item_total, 1 + k_cols)
    row_block = recv_labels[:, 0]
    order = jnp.argsort(row_block).astype(jnp.int32)
    counts = jnp.sum(row_block[:, None] == jnp.arange(n_scan)[None, :], axis=0)
    starts = jnp.concatenate([jnp.zeros((1,), jnp.int32), jnp.cumsum(counts).astype(jnp.int32)])
    return place(recv_rows, order, starts, recv_labels[:, 1], n_scan, n_tile)


def place(recv, order, starts, col_block, n_rows, n_cols):
    items, tile_pixels, _ = recv.shape

    group = 4 if n_rows % 4 == 0 else 1

    def kernel(order_ref, starts_ref, col_ref, recv_ref, out_ref):
        r = pl.program_id(0)
        out_ref[...] = jnp.zeros(out_ref.shape, out_ref.dtype)
        for q in range(group):

            def body(k, carry, q=q):
                i = order_ref[k]
                at = pl.ds(pl.multiple_of(col_ref[i] * tile_pixels, tile_pixels), tile_pixels)
                out_ref[q * tile_pixels : (q + 1) * tile_pixels, at] += recv_ref[i]
                return carry

            lax.fori_loop(starts_ref[r * group + q], starts_ref[r * group + q + 1], body, 0)

    return pl.pallas_call(
        kernel,
        grid_spec=pltpu.PrefetchScalarGridSpec(
            num_scalar_prefetch=3,
            grid=(n_rows // group,),
            in_specs=[pl.BlockSpec((items, tile_pixels, tile_pixels), lambda r, a, b, c: (0, 0, 0))],
            out_specs=pl.BlockSpec((group * tile_pixels, n_cols * tile_pixels), lambda r, a, b, c: (r, 0)),
        ),
        out_shape=jax.ShapeDtypeStruct((n_rows * tile_pixels, n_cols * tile_pixels), jnp.float32),
    )(order, starts, col_block, recv)


def solution(mesh):
    devices = mesh.devices.transpose([mesh.axis_names.index("scan"), mesh.axis_names.index("tile")])
    n_scan, n_tile = devices.shape
    n_sx = 4 if n_scan % 4 == 0 else 1
    sub = Mesh(devices.reshape(n_scan // n_sx, n_sx, n_tile), ("sy", "sx", "tile"))
    return jax.shard_map(
        per_device,
        mesh=sub,
        in_specs=(
            P("tile", SCAN_AXES, None),
            P("tile", SCAN_AXES),
            P("tile"),
            P("tile"),
            P("tile", None),
            P(),
        ),
        out_specs=P("tile", SCAN_AXES),
        check_vma=False,
    )
```

```python
import jax
import jax.numpy as jnp
from jax import lax
from jax.experimental import pallas as pl
from jax.experimental.pallas import tpu as pltpu
from jax.sharding import Mesh, PartitionSpec as P

DEG_MAX = 8
NGB = 24
SCAN_AXES = ("sy", "sx")


def build_templates(ground_rows, position, lengths, degrees):
    position = position.astype(jnp.float32)
    length_value = lengths.astype(jnp.float32)[:, None]
    inside = position[None, :] < length_value
    coord = 2.0 * (position[None, :] + 0.5) / length_value - 1.0
    columns = []
    previous = jnp.ones_like(coord)
    current = coord
    for degree in range(1, DEG_MAX + 1):
        keep = jnp.logical_and(inside, (degree <= degrees)[:, None])
        columns.append(jnp.where(keep, current, jnp.float32(0.0)))
        following = ((2.0 * degree + 1.0) * coord * current - degree * previous) / (degree + 1.0)
        previous, current = (current, following)
    poly_part = jnp.stack(columns, axis=2)
    bins = jnp.logical_and(
        ground_rows[:, :, None] == jnp.arange(NGB)[None, None, :], inside[:, :, None]
    ).astype(jnp.float32)
    return jnp.concatenate([poly_part, bins], axis=2).astype(jnp.bfloat16)


def per_device(pointing, ground_bin, degrees, lengths, tile_lists, owner_map):
    scan_count, sample_rows, width = pointing.shape
    n_sy = lax.axis_size("sy")
    n_sx = lax.axis_size("sx")
    n_scan = n_sy * n_sx
    n_tile = lax.axis_size("tile")
    sy = lax.axis_index("sy")
    sx = lax.axis_index("sx")
    scan_index = sy * n_sx + sx
    k_tiles = tile_lists.shape[1]
    tile_pixels = width // k_tiles
    col_width = tile_pixels
    half = k_tiles // 2 + 1
    template_cols = DEG_MAX + NGB

    position = scan_index * sample_rows + jnp.arange(sample_rows)
    inside = position[None, :] < lengths[:, None]
    masked = jnp.where(inside[:, :, None], pointing, jnp.zeros_like(pointing))
    template = build_templates(ground_bin, position, lengths, degrees)
    pad = jnp.zeros((scan_count, sample_rows, tile_pixels - template_cols), jnp.bfloat16)
    local = jnp.concatenate([masked, template, pad], axis=2)

    def shifted(x, axis, n, d):
        return lax.ppermute(x, axis, [(i, (i + d) % n) for i in range(n)])

    def column_sums(one, gather_axis, n_gather, reduce_axis, n_reduce, reduce_index):
        rows_all = jnp.concatenate(
            [one] + [shifted(one, gather_axis, n_gather, d) for d in range(1, n_gather)], axis=1
        )
        rows = rows_all[:, :, :width]
        tpl = rows_all[:, :, width : width + template_cols]
        if reduce_axis == "sy":
            firsts = [((reduce_index + d) % n_reduce) * n_sx + sx for d in range(n_reduce)]
        else:
            firsts = [sy * n_sx + (reduce_index + d) % n_reduce for d in range(n_reduce)]
        cols = jnp.concatenate(
            [lax.dynamic_slice_in_dim(rows, f * tile_pixels, tile_pixels, 2) for f in firsts], axis=2
        )
        grams = jnp.einsum("snp,snq->pq", rows, cols, preferred_element_type=jnp.float32)
        projs = jnp.einsum("snt,snp->tp", tpl, rows, preferred_element_type=jnp.float32)
        projs = jnp.swapaxes(projs.reshape(template_cols, k_tiles, tile_pixels), 0, 1)
        projs = projs.reshape(k_tiles * template_cols, tile_pixels)
        summed = None
        for d in range(n_reduce):
            part = jnp.concatenate([grams[:, d * col_width : (d + 1) * col_width], projs], axis=0)
            part = part if d == 0 else shifted(part, reduce_axis, n_reduce, d)
            summed = part if summed is None else summed + part
        norm = jnp.einsum("snt,snu->tu", tpl, tpl, preferred_element_type=jnp.float32)
        norm = norm + sum(shifted(norm, reduce_axis, n_reduce, d) for d in range(1, n_reduce))
        return summed, norm

    first = column_sums(local[0:1], "sx", n_sx, "sy", n_sy, sy)
    second = column_sums(local[1:2], "sy", n_sy, "sx", n_sx, sx)
    summed = jnp.stack([first[0], second[0]])
    normal = jnp.stack([first[1], second[1]]) + jnp.eye(template_cols, dtype=jnp.float32)[None]
    factor = jnp.linalg.cholesky(normal)
    eye = jnp.broadcast_to(jnp.eye(template_cols, dtype=jnp.float32), normal.shape)
    inverse = jax.scipy.linalg.solve_triangular(factor, eye, lower=True)
    gram = summed[:, :width]
    proj = summed[:, width : width + k_tiles * template_cols].reshape(scan_count, k_tiles, template_cols, tile_pixels)
    proj = jnp.swapaxes(proj, 1, 2).reshape(scan_count, template_cols, width)
    whitened = jnp.einsum("stu,sup->stp", inverse, proj, precision=lax.Precision.HIGHEST)
    w_col = lax.dynamic_slice_in_dim(whitened, scan_index * tile_pixels, tile_pixels, 2)
    correction = jnp.einsum("stp,stq->spq", whitened, w_col, precision=lax.Precision.HIGHEST)
    contrib = gram - correction

    k_cols = 1
    tile_rows = contrib.reshape(scan_count * k_tiles, tile_pixels, col_width)
    row_tiles = tile_lists.reshape(-1)
    matches = row_tiles[:, None] == jnp.arange(owner_map.shape[0])[None, :]
    owners = jnp.sum(jnp.where(matches, owner_map[None, :], 0), axis=1)
    row_total = scan_count * k_tiles
    capacity = row_total // n_tile
    ordering = jnp.argsort(owners * row_total + jnp.arange(row_total), stable=True)
    local_cols = (
        lax.dynamic_slice_in_dim(tile_lists, scan_index * k_cols, k_cols, 1) - scan_index * n_tile
    )
    local_cols = jnp.repeat(local_cols, k_tiles, axis=0)
    labels = jnp.concatenate([(row_tiles // n_tile)[:, None], local_cols], axis=1)
    send_rows = tile_rows[ordering].reshape(n_tile, capacity, tile_pixels, col_width)
    send_labels = labels[ordering].reshape(n_tile, capacity, 1 + k_cols)
    recv_rows, recv_labels = (
        lax.all_to_all(send_rows, "tile", split_axis=0, concat_axis=0, tiled=True),
        lax.all_to_all(send_labels, "tile", split_axis=0, concat_axis=0, tiled=True),
    )
    item_total = n_tile * capacity
    recv_rows = recv_rows.reshape(item_total, tile_pixels, tile_pixels)
    recv_labels = recv_labels.reshape(item_total, 1 + k_cols)
    row_block = recv_labels[:, 0]
    order = jnp.argsort(row_block).astype(jnp.int32)
    counts = jnp.sum(row_block[:, None] == jnp.arange(n_scan)[None, :], axis=0)
    starts = jnp.concatenate([jnp.zeros((1,), jnp.int32), jnp.cumsum(counts).astype(jnp.int32)])
    return place(recv_rows, order, starts, recv_labels[:, 1], n_scan, n_tile)


def place(recv, order, starts, col_block, n_rows, n_cols):
    items, tile_pixels, _ = recv.shape

    group = 4 if n_rows % 4 == 0 else 1

    def kernel(order_ref, starts_ref, col_ref, recv_ref, out_ref):
        r = pl.program_id(0)
        out_ref[...] = jnp.zeros(out_ref.shape, out_ref.dtype)
        for q in range(group):

            def body(k, carry, q=q):
                i = order_ref[k]
                at = pl.ds(pl.multiple_of(col_ref[i] * tile_pixels, tile_pixels), tile_pixels)
                out_ref[q * tile_pixels : (q + 1) * tile_pixels, at] += recv_ref[i]
                return carry

            lax.fori_loop(starts_ref[r * group + q], starts_ref[r * group + q + 1], body, 0)

    return pl.pallas_call(
        kernel,
        grid_spec=pltpu.PrefetchScalarGridSpec(
            num_scalar_prefetch=3,
            grid=(n_rows // group,),
            in_specs=[pl.BlockSpec((items, tile_pixels, tile_pixels), lambda r, a, b, c: (0, 0, 0))],
            out_specs=pl.BlockSpec((group * tile_pixels, n_cols * tile_pixels), lambda r, a, b, c: (r, 0)),
        ),
        out_shape=jax.ShapeDtypeStruct((n_rows * tile_pixels, n_cols * tile_pixels), jnp.float32),
    )(order, starts, col_block, recv)


def solution(mesh):
    devices = mesh.devices.transpose([mesh.axis_names.index("scan"), mesh.axis_names.index("tile")])
    n_scan, n_tile = devices.shape
    n_sx = 4 if n_scan % 4 == 0 else 1
    sub = Mesh(devices.reshape(n_scan // n_sx, n_sx, n_tile), ("sy", "sx", "tile"))
    return jax.shard_map(
        per_device,
        mesh=sub,
        in_specs=(
            P("tile", SCAN_AXES, None),
            P("tile", SCAN_AXES),
            P("tile"),
            P("tile"),
            P("tile", None),
            P(),
        ),
        out_specs=P("tile", SCAN_AXES),
        check_vma=False,
    )
```

```python
import jax
import jax.numpy as jnp
from jax import lax
from jax.experimental import pallas as pl
from jax.experimental.pallas import tpu as pltpu
from jax.sharding import Mesh, PartitionSpec as P

DEG_MAX = 8
NGB = 24
SCAN_AXES = ("sy", "sx")


def build_templates(ground_rows, position, lengths, degrees):
    position = position.astype(jnp.float32)
    length_value = lengths.astype(jnp.float32)[:, None]
    inside = position[None, :] < length_value
    coord = 2.0 * (position[None, :] + 0.5) / length_value - 1.0
    columns = []
    previous = jnp.ones_like(coord)
    current = coord
    for degree in range(1, DEG_MAX + 1):
        keep = jnp.logical_and(inside, (degree <= degrees)[:, None])
        columns.append(jnp.where(keep, current, jnp.float32(0.0)))
        following = ((2.0 * degree + 1.0) * coord * current - degree * previous) / (degree + 1.0)
        previous, current = (current, following)
    poly_part = jnp.stack(columns, axis=2)
    bins = jnp.logical_and(
        ground_rows[:, :, None] == jnp.arange(NGB)[None, None, :], inside[:, :, None]
    ).astype(jnp.float32)
    return jnp.concatenate([poly_part, bins], axis=2).astype(jnp.bfloat16)


def per_device(pointing, ground_bin, degrees, lengths, tile_lists, owner_map):
    scan_count, sample_rows, width = pointing.shape
    n_sy = lax.axis_size("sy")
    n_sx = lax.axis_size("sx")
    n_scan = n_sy * n_sx
    n_tile = lax.axis_size("tile")
    sy = lax.axis_index("sy")
    sx = lax.axis_index("sx")
    scan_index = sy * n_sx + sx
    k_tiles = tile_lists.shape[1]
    tile_pixels = width // k_tiles
    col_width = tile_pixels
    half = k_tiles // 2 + 1
    template_cols = DEG_MAX + NGB

    position = scan_index * sample_rows + jnp.arange(sample_rows)
    inside = position[None, :] < lengths[:, None]
    masked = jnp.where(inside[:, :, None], pointing, jnp.zeros_like(pointing))
    template = build_templates(ground_bin, position, lengths, degrees)
    pad = jnp.zeros((scan_count, sample_rows, tile_pixels - template_cols), jnp.bfloat16)
    local = jnp.concatenate([masked, template, pad], axis=2)

    def shifted(x, axis, n, d):
        return lax.ppermute(x, axis, [(i, (i + d) % n) for i in range(n)])

    def column_sums(one, gather_axis, n_gather, reduce_axis, n_reduce, reduce_index):
        rows_all = jnp.concatenate(
            [one] + [shifted(one, gather_axis, n_gather, d) for d in range(1, n_gather)], axis=1
        )
        rows = rows_all[:, :, :width]
        tpl = rows_all[:, :, width : width + template_cols]
        if reduce_axis == "sy":
            firsts = [((reduce_index + d) % n_reduce) * n_sx + sx for d in range(n_reduce)]
        else:
            firsts = [sy * n_sx + (reduce_index + d) % n_reduce for d in range(n_reduce)]
        cols = jnp.concatenate(
            [lax.dynamic_slice_in_dim(rows, f * tile_pixels, tile_pixels, 2) for f in firsts], axis=2
        )
        grams = jnp.einsum("snp,snq->pq", rows, cols, preferred_element_type=jnp.float32)
        projs = jnp.einsum("snt,snp->tp", tpl, rows, preferred_element_type=jnp.float32)
        projs = jnp.swapaxes(projs.reshape(template_cols, k_tiles, tile_pixels), 0, 1)
        projs = projs.reshape(k_tiles * template_cols, tile_pixels)
        summed = None
        for d in range(n_reduce):
            part = jnp.concatenate([grams[:, d * col_width : (d + 1) * col_width], projs], axis=0)
            part = part if d == 0 else shifted(part, reduce_axis, n_reduce, d)
            summed = part if summed is None else summed + part
        norm = jnp.einsum("snt,snu->tu", tpl, tpl, preferred_element_type=jnp.float32)
        norm = norm + sum(shifted(norm, reduce_axis, n_reduce, d) for d in range(1, n_reduce))
        return summed, norm

    first = column_sums(local[0:1], "sx", n_sx, "sy", n_sy, sy)
    second = column_sums(local[1:2], "sy", n_sy, "sx", n_sx, sx)
    summed = jnp.stack([first[0], second[0]])
    normal = jnp.stack([first[1], second[1]]) + jnp.eye(template_cols, dtype=jnp.float32)[None]
    factor = jnp.linalg.cholesky(normal)
    eye = jnp.broadcast_to(jnp.eye(template_cols, dtype=jnp.float32), normal.shape)
    inverse = jax.scipy.linalg.solve_triangular(factor, eye, lower=True)
    gram = summed[:, :width]
    proj = summed[:, width : width + k_tiles * template_cols].reshape(scan_count, k_tiles, template_cols, tile_pixels)
    proj = jnp.swapaxes(proj, 1, 2).reshape(scan_count, template_cols, width)
    whitened = jnp.einsum("stu,sup->stp", inverse, proj, precision=lax.Precision.HIGH)
    w_col = lax.dynamic_slice_in_dim(whitened, scan_index * tile_pixels, tile_pixels, 2)
    correction = jnp.einsum("stp,stq->spq", whitened, w_col, precision=lax.Precision.HIGH)
    contrib = gram - correction

    k_cols = 1
    tile_rows = contrib.reshape(scan_count * k_tiles, tile_pixels, col_width)
    row_tiles = tile_lists.reshape(-1)
    matches = row_tiles[:, None] == jnp.arange(owner_map.shape[0])[None, :]
    owners = jnp.sum(jnp.where(matches, owner_map[None, :], 0), axis=1)
    row_total = scan_count * k_tiles
    capacity = row_total // n_tile
    ordering = jnp.argsort(owners * row_total + jnp.arange(row_total), stable=True)
    local_cols = (
        lax.dynamic_slice_in_dim(tile_lists, scan_index * k_cols, k_cols, 1) - scan_index * n_tile
    )
    local_cols = jnp.repeat(local_cols, k_tiles, axis=0)
    labels = jnp.concatenate([(row_tiles // n_tile)[:, None], local_cols], axis=1)
    send_rows = tile_rows[ordering].reshape(n_tile, capacity, tile_pixels, col_width)
    send_labels = labels[ordering].reshape(n_tile, capacity, 1 + k_cols)
    recv_rows, recv_labels = (
        lax.all_to_all(send_rows, "tile", split_axis=0, concat_axis=0, tiled=True),
        lax.all_to_all(send_labels, "tile", split_axis=0, concat_axis=0, tiled=True),
    )
    item_total = n_tile * capacity
    recv_rows = recv_rows.reshape(item_total, tile_pixels, tile_pixels)
    recv_labels = recv_labels.reshape(item_total, 1 + k_cols)
    row_block = recv_labels[:, 0]
    order = jnp.argsort(row_block).astype(jnp.int32)
    counts = jnp.sum(row_block[:, None] == jnp.arange(n_scan)[None, :], axis=0)
    starts = jnp.concatenate([jnp.zeros((1,), jnp.int32), jnp.cumsum(counts).astype(jnp.int32)])
    return place(recv_rows, order, starts, recv_labels[:, 1], n_scan, n_tile)


def place(recv, order, starts, col_block, n_rows, n_cols):
    items, tile_pixels, _ = recv.shape

    group = 4 if n_rows % 4 == 0 else 1

    def kernel(order_ref, starts_ref, col_ref, recv_ref, out_ref):
        r = pl.program_id(0)
        out_ref[...] = jnp.zeros(out_ref.shape, out_ref.dtype)
        for q in range(group):

            def body(k, carry, q=q):
                i = order_ref[k]
                at = pl.ds(pl.multiple_of(col_ref[i] * tile_pixels, tile_pixels), tile_pixels)
                out_ref[q * tile_pixels : (q + 1) * tile_pixels, at] += recv_ref[i]
                return carry

            lax.fori_loop(starts_ref[r * group + q], starts_ref[r * group + q + 1], body, 0)

    return pl.pallas_call(
        kernel,
        grid_spec=pltpu.PrefetchScalarGridSpec(
            num_scalar_prefetch=3,
            grid=(n_rows // group,),
            in_specs=[pl.BlockSpec((items, tile_pixels, tile_pixels), lambda r, a, b, c: (0, 0, 0))],
            out_specs=pl.BlockSpec((group * tile_pixels, n_cols * tile_pixels), lambda r, a, b, c: (r, 0)),
        ),
        out_shape=jax.ShapeDtypeStruct((n_rows * tile_pixels, n_cols * tile_pixels), jnp.float32),
    )(order, starts, col_block, recv)


def solution(mesh):
    devices = mesh.devices.transpose([mesh.axis_names.index("scan"), mesh.axis_names.index("tile")])
    n_scan, n_tile = devices.shape
    n_sx = 4 if n_scan % 4 == 0 else 1
    sub = Mesh(devices.reshape(n_scan // n_sx, n_sx, n_tile), ("sy", "sx", "tile"))
    return jax.shard_map(
        per_device,
        mesh=sub,
        in_specs=(
            P("tile", SCAN_AXES, None),
            P("tile", SCAN_AXES),
            P("tile"),
            P("tile"),
            P("tile", None),
            P(),
        ),
        out_specs=P("tile", SCAN_AXES),
        check_vma=False,
    )
```

```python
import jax
import jax.numpy as jnp
from jax import lax
from jax.experimental import pallas as pl
from jax.experimental.pallas import tpu as pltpu
from jax.sharding import Mesh, PartitionSpec as P

DEG_MAX = 8
NGB = 24
SCAN_AXES = ("sy", "sx")


def build_templates(ground_rows, position, lengths, degrees, block):
    position = position.astype(jnp.float32)
    length_value = lengths.astype(jnp.float32)[:, None]
    inside = position[None, :] < length_value
    coord = 2.0 * (position[None, :] + 0.5) / length_value - 1.0
    column = jnp.arange(block)[None, None, :]
    out = jnp.zeros(ground_rows.shape + (block,), jnp.float32)
    previous = jnp.ones_like(coord)
    current = coord
    for degree in range(1, DEG_MAX + 1):
        keep = jnp.logical_and(inside, (degree <= degrees)[:, None])
        value = jnp.where(keep, current, jnp.float32(0.0))
        out = jnp.where(column == degree - 1, value[:, :, None], out)
        following = ((2.0 * degree + 1.0) * coord * current - degree * previous) / (degree + 1.0)
        previous, current = (current, following)
    hit = jnp.logical_and(ground_rows[:, :, None] + DEG_MAX == column, inside[:, :, None])
    hit = jnp.logical_and(hit, column < DEG_MAX + NGB)
    out = jnp.where(hit, jnp.float32(1.0), out)
    return out.astype(jnp.bfloat16)


def per_device(pointing, ground_bin, degrees, lengths, tile_lists, owner_map):
    scan_count, sample_rows, width = pointing.shape
    n_sy = lax.axis_size("sy")
    n_sx = lax.axis_size("sx")
    n_scan = n_sy * n_sx
    n_tile = lax.axis_size("tile")
    sy = lax.axis_index("sy")
    sx = lax.axis_index("sx")
    scan_index = sy * n_sx + sx
    k_tiles = tile_lists.shape[1]
    tile_pixels = width // k_tiles
    col_width = tile_pixels
    half = k_tiles // 2 + 1
    template_cols = DEG_MAX + NGB

    position = scan_index * sample_rows + jnp.arange(sample_rows)
    inside = position[None, :] < lengths[:, None]
    masked = jnp.where(inside[:, :, None], pointing, jnp.zeros_like(pointing))
    template = build_templates(ground_bin, position, lengths, degrees, tile_pixels)
    local = jnp.concatenate([masked, template], axis=2)

    def shifted(x, axis, n, d):
        return lax.ppermute(x, axis, [(i, (i + d) % n) for i in range(n)])

    def column_sums(one, gather_axis, n_gather, reduce_axis, n_reduce, reduce_index):
        rows_all = jnp.concatenate(
            [one] + [shifted(one, gather_axis, n_gather, d) for d in range(1, n_gather)], axis=1
        )
        rows = rows_all[:, :, :width]
        tpl = rows_all[:, :, width : width + template_cols]
        if reduce_axis == "sy":
            firsts = [((reduce_index + d) % n_reduce) * n_sx + sx for d in range(n_reduce)]
        else:
            firsts = [sy * n_sx + (reduce_index + d) % n_reduce for d in range(n_reduce)]
        cols = jnp.concatenate(
            [lax.dynamic_slice_in_dim(rows, f * tile_pixels, tile_pixels, 2) for f in firsts], axis=2
        )
        grams = jnp.einsum("snp,snq->pq", rows, cols, preferred_element_type=jnp.float32)
        projs = jnp.einsum("snt,snp->tp", tpl, rows, preferred_element_type=jnp.float32)
        projs = jnp.swapaxes(projs.reshape(template_cols, k_tiles, tile_pixels), 0, 1)
        projs = projs.reshape(k_tiles * template_cols, tile_pixels)
        summed = None
        for d in range(n_reduce):
            part = jnp.concatenate([grams[:, d * col_width : (d + 1) * col_width], projs], axis=0)
            part = part if d == 0 else shifted(part, reduce_axis, n_reduce, d)
            summed = part if summed is None else summed + part
        norm = jnp.einsum("snt,snu->tu", tpl, tpl, preferred_element_type=jnp.float32)
        norm = norm + sum(shifted(norm, reduce_axis, n_reduce, d) for d in range(1, n_reduce))
        return summed, norm

    first = column_sums(local[0:1], "sx", n_sx, "sy", n_sy, sy)
    second = column_sums(local[1:2], "sy", n_sy, "sx", n_sx, sx)
    summed = jnp.stack([first[0], second[0]])
    normal = jnp.stack([first[1], second[1]]) + jnp.eye(template_cols, dtype=jnp.float32)[None]
    factor = jnp.linalg.cholesky(normal)
    eye = jnp.broadcast_to(jnp.eye(template_cols, dtype=jnp.float32), normal.shape)
    inverse = jax.scipy.linalg.solve_triangular(factor, eye, lower=True)
    gram = summed[:, :width]
    proj = summed[:, width : width + k_tiles * template_cols].reshape(scan_count, k_tiles, template_cols, tile_pixels)
    proj = jnp.swapaxes(proj, 1, 2).reshape(scan_count, template_cols, width)
    whitened = jnp.einsum("stu,sup->stp", inverse, proj, precision=lax.Precision.HIGH)
    w_col = lax.dynamic_slice_in_dim(whitened, scan_index * tile_pixels, tile_pixels, 2)
    correction = jnp.einsum("stp,stq->spq", whitened, w_col, precision=lax.Precision.HIGH)
    contrib = gram - correction

    k_cols = 1
    tile_rows = contrib.reshape(scan_count * k_tiles, tile_pixels, col_width)
    row_tiles = tile_lists.reshape(-1)
    matches = row_tiles[:, None] == jnp.arange(owner_map.shape[0])[None, :]
    owners = jnp.sum(jnp.where(matches, owner_map[None, :], 0), axis=1)
    row_total = scan_count * k_tiles
    capacity = row_total // n_tile
    ordering = jnp.argsort(owners * row_total + jnp.arange(row_total), stable=True)
    local_cols = (
        lax.dynamic_slice_in_dim(tile_lists, scan_index * k_cols, k_cols, 1) - scan_index * n_tile
    )
    local_cols = jnp.repeat(local_cols, k_tiles, axis=0)
    labels = jnp.concatenate([(row_tiles // n_tile)[:, None], local_cols], axis=1)
    send_rows = tile_rows[ordering].reshape(n_tile, capacity, tile_pixels, col_width)
    send_labels = labels[ordering].reshape(n_tile, capacity, 1 + k_cols)
    recv_rows, recv_labels = (
        lax.all_to_all(send_rows, "tile", split_axis=0, concat_axis=0, tiled=True),
        lax.all_to_all(send_labels, "tile", split_axis=0, concat_axis=0, tiled=True),
    )
    item_total = n_tile * capacity
    recv_rows = recv_rows.reshape(item_total, tile_pixels, tile_pixels)
    recv_labels = recv_labels.reshape(item_total, 1 + k_cols)
    row_block = recv_labels[:, 0]
    order = jnp.argsort(row_block).astype(jnp.int32)
    counts = jnp.sum(row_block[:, None] == jnp.arange(n_scan)[None, :], axis=0)
    starts = jnp.concatenate([jnp.zeros((1,), jnp.int32), jnp.cumsum(counts).astype(jnp.int32)])
    return place(recv_rows, order, starts, recv_labels[:, 1], n_scan, n_tile)


def place(recv, order, starts, col_block, n_rows, n_cols):
    items, tile_pixels, _ = recv.shape

    group = 4 if n_rows % 4 == 0 else 1

    def kernel(order_ref, starts_ref, col_ref, recv_ref, out_ref):
        r = pl.program_id(0)
        out_ref[...] = jnp.zeros(out_ref.shape, out_ref.dtype)
        for q in range(group):

            def body(k, carry, q=q):
                i = order_ref[k]
                at = pl.ds(pl.multiple_of(col_ref[i] * tile_pixels, tile_pixels), tile_pixels)
                out_ref[q * tile_pixels : (q + 1) * tile_pixels, at] += recv_ref[i]
                return carry

            lax.fori_loop(starts_ref[r * group + q], starts_ref[r * group + q + 1], body, 0)

    return pl.pallas_call(
        kernel,
        grid_spec=pltpu.PrefetchScalarGridSpec(
            num_scalar_prefetch=3,
            grid=(n_rows // group,),
            in_specs=[pl.BlockSpec((items, tile_pixels, tile_pixels), lambda r, a, b, c: (0, 0, 0))],
            out_specs=pl.BlockSpec((group * tile_pixels, n_cols * tile_pixels), lambda r, a, b, c: (r, 0)),
        ),
        out_shape=jax.ShapeDtypeStruct((n_rows * tile_pixels, n_cols * tile_pixels), jnp.float32),
    )(order, starts, col_block, recv)


def solution(mesh):
    devices = mesh.devices.transpose([mesh.axis_names.index("scan"), mesh.axis_names.index("tile")])
    n_scan, n_tile = devices.shape
    n_sx = 4 if n_scan % 4 == 0 else 1
    sub = Mesh(devices.reshape(n_scan // n_sx, n_sx, n_tile), ("sy", "sx", "tile"))
    return jax.shard_map(
        per_device,
        mesh=sub,
        in_specs=(
            P("tile", SCAN_AXES, None),
            P("tile", SCAN_AXES),
            P("tile"),
            P("tile"),
            P("tile", None),
            P(),
        ),
        out_specs=P("tile", SCAN_AXES),
        check_vma=False,
    )
```

```python
import jax
import jax.numpy as jnp
from jax import lax
from jax.experimental import pallas as pl
from jax.experimental.pallas import tpu as pltpu
from jax.sharding import Mesh, PartitionSpec as P

DEG_MAX = 8
NGB = 24
SCAN_AXES = ("sy", "sx")


def build_templates(ground_rows, position, lengths, degrees, block):
    position = position.astype(jnp.float32)
    length_value = lengths.astype(jnp.float32)[:, None]
    inside = position[None, :] < length_value
    coord = 2.0 * (position[None, :] + 0.5) / length_value - 1.0
    column = jnp.arange(block)[None, None, :]
    out = jnp.zeros(ground_rows.shape + (block,), jnp.float32)
    previous = jnp.ones_like(coord)
    current = coord
    for degree in range(1, DEG_MAX + 1):
        keep = jnp.logical_and(inside, (degree <= degrees)[:, None])
        value = jnp.where(keep, current, jnp.float32(0.0))
        out = jnp.where(column == degree - 1, value[:, :, None], out)
        following = ((2.0 * degree + 1.0) * coord * current - degree * previous) / (degree + 1.0)
        previous, current = (current, following)
    hit = jnp.logical_and(ground_rows[:, :, None] + DEG_MAX == column, inside[:, :, None])
    hit = jnp.logical_and(hit, column < DEG_MAX + NGB)
    out = jnp.where(hit, jnp.float32(1.0), out)
    return out.astype(jnp.bfloat16)


def per_device(pointing, ground_bin, degrees, lengths, tile_lists, owner_map):
    scan_count, sample_rows, width = pointing.shape
    n_sy = lax.axis_size("sy")
    n_sx = lax.axis_size("sx")
    n_scan = n_sy * n_sx
    n_tile = lax.axis_size("tile")
    sy = lax.axis_index("sy")
    sx = lax.axis_index("sx")
    scan_index = sy * n_sx + sx
    k_tiles = tile_lists.shape[1]
    tile_pixels = width // k_tiles
    col_width = tile_pixels
    half = k_tiles // 2 + 1
    template_cols = DEG_MAX + NGB

    position = scan_index * sample_rows + jnp.arange(sample_rows)
    inside = position[None, :] < lengths[:, None]
    masked = jnp.where(inside[:, :, None], pointing, jnp.zeros_like(pointing))
    template = build_templates(ground_bin, position, lengths, degrees, tile_pixels)
    both = template[0:1] + jnp.roll(template[1:2], template_cols, axis=2)
    local_first = jnp.concatenate([masked[0:1], both], axis=2)
    local_second = jnp.concatenate([masked[1:2], template[1:2]], axis=2)

    def shifted(x, axis, n, d):
        return lax.ppermute(x, axis, [(i, (i + d) % n) for i in range(n)])

    def column_sums(one, gather_axis, n_gather, reduce_axis, n_reduce, reduce_index, normals):
        rows_all = jnp.concatenate(
            [one] + [shifted(one, gather_axis, n_gather, d) for d in range(1, n_gather)], axis=1
        )
        rows = rows_all[:, :, :width]
        tpl = rows_all[:, :, width : width + template_cols]
        if reduce_axis == "sy":
            firsts = [((reduce_index + d) % n_reduce) * n_sx + sx for d in range(n_reduce)]
        else:
            firsts = [sy * n_sx + (reduce_index + d) % n_reduce for d in range(n_reduce)]
        cols = jnp.concatenate(
            [lax.dynamic_slice_in_dim(rows, f * tile_pixels, tile_pixels, 2) for f in firsts], axis=2
        )
        grams = jnp.einsum("snp,snq->pq", rows, cols, preferred_element_type=jnp.float32)
        projs = jnp.einsum("snt,snp->tp", tpl, rows, preferred_element_type=jnp.float32)
        projs = jnp.swapaxes(projs.reshape(template_cols, k_tiles, tile_pixels), 0, 1)
        projs = projs.reshape(k_tiles * template_cols, tile_pixels)
        extra = []
        for k in range(normals):
            other = rows_all[:, :, width + k * template_cols : width + (k + 1) * template_cols]
            norm = jnp.einsum("snt,snu->tu", other, other, preferred_element_type=jnp.float32)
            extra.append(jnp.pad(norm, ((0, 0), (0, col_width - template_cols))))
        summed = None
        for d in range(n_reduce):
            part = jnp.concatenate([grams[:, d * col_width : (d + 1) * col_width], projs] + extra, axis=0)
            part = part if d == 0 else shifted(part, reduce_axis, n_reduce, d)
            summed = part if summed is None else summed + part
        return summed

    first = column_sums(local_first, "sx", n_sx, "sy", n_sy, sy, scan_count)
    second = column_sums(local_second, "sy", n_sy, "sx", n_sx, sx, 0)
    rows_main = width + k_tiles * template_cols
    summed = jnp.stack([first[:rows_main], second])
    normal = first[rows_main:].reshape(scan_count, template_cols, col_width)[:, :, :template_cols]
    normal = normal + jnp.eye(template_cols, dtype=jnp.float32)[None]
    factor = jnp.linalg.cholesky(normal)
    eye = jnp.broadcast_to(jnp.eye(template_cols, dtype=jnp.float32), normal.shape)
    inverse = jax.scipy.linalg.solve_triangular(factor, eye, lower=True)
    gram = summed[:, :width]
    proj = summed[:, width : width + k_tiles * template_cols].reshape(scan_count, k_tiles, template_cols, tile_pixels)
    proj = jnp.swapaxes(proj, 1, 2).reshape(scan_count, template_cols, width)
    whitened = jnp.einsum("stu,sup->stp", inverse, proj, precision=lax.Precision.HIGH)
    w_col = lax.dynamic_slice_in_dim(whitened, scan_index * tile_pixels, tile_pixels, 2)
    correction = jnp.einsum("stp,stq->spq", whitened, w_col, precision=lax.Precision.HIGH)
    contrib = gram - correction

    k_cols = 1
    tile_rows = contrib.reshape(scan_count * k_tiles, tile_pixels, col_width)
    row_tiles = tile_lists.reshape(-1)
    matches = row_tiles[:, None] == jnp.arange(owner_map.shape[0])[None, :]
    owners = jnp.sum(jnp.where(matches, owner_map[None, :], 0), axis=1)
    row_total = scan_count * k_tiles
    capacity = row_total // n_tile
    ordering = jnp.argsort(owners * row_total + jnp.arange(row_total), stable=True)
    local_cols = (
        lax.dynamic_slice_in_dim(tile_lists, scan_index * k_cols, k_cols, 1) - scan_index * n_tile
    )
    local_cols = jnp.repeat(local_cols, k_tiles, axis=0)
    labels = jnp.concatenate([(row_tiles // n_tile)[:, None], local_cols], axis=1)
    send_rows = tile_rows[ordering].reshape(n_tile, capacity, tile_pixels, col_width)
    send_labels = labels[ordering].reshape(n_tile, capacity, 1 + k_cols)
    recv_rows, recv_labels = (
        lax.all_to_all(send_rows, "tile", split_axis=0, concat_axis=0, tiled=True),
        lax.all_to_all(send_labels, "tile", split_axis=0, concat_axis=0, tiled=True),
    )
    item_total = n_tile * capacity
    recv_rows = recv_rows.reshape(item_total, tile_pixels, tile_pixels)
    recv_labels = recv_labels.reshape(item_total, 1 + k_cols)
    row_block = recv_labels[:, 0]
    order = jnp.argsort(row_block).astype(jnp.int32)
    counts = jnp.sum(row_block[:, None] == jnp.arange(n_scan)[None, :], axis=0)
    starts = jnp.concatenate([jnp.zeros((1,), jnp.int32), jnp.cumsum(counts).astype(jnp.int32)])
    return place(recv_rows, order, starts, recv_labels[:, 1], n_scan, n_tile)


def place(recv, order, starts, col_block, n_rows, n_cols):
    items, tile_pixels, _ = recv.shape

    group = 4 if n_rows % 4 == 0 else 1

    def kernel(order_ref, starts_ref, col_ref, recv_ref, out_ref):
        r = pl.program_id(0)
        out_ref[...] = jnp.zeros(out_ref.shape, out_ref.dtype)
        for q in range(group):

            def body(k, carry, q=q):
                i = order_ref[k]
                at = pl.ds(pl.multiple_of(col_ref[i] * tile_pixels, tile_pixels), tile_pixels)
                out_ref[q * tile_pixels : (q + 1) * tile_pixels, at] += recv_ref[i]
                return carry

            lax.fori_loop(starts_ref[r * group + q], starts_ref[r * group + q + 1], body, 0)

    return pl.pallas_call(
        kernel,
        grid_spec=pltpu.PrefetchScalarGridSpec(
            num_scalar_prefetch=3,
            grid=(n_rows // group,),
            in_specs=[pl.BlockSpec((items, tile_pixels, tile_pixels), lambda r, a, b, c: (0, 0, 0))],
            out_specs=pl.BlockSpec((group * tile_pixels, n_cols * tile_pixels), lambda r, a, b, c: (r, 0)),
        ),
        out_shape=jax.ShapeDtypeStruct((n_rows * tile_pixels, n_cols * tile_pixels), jnp.float32),
    )(order, starts, col_block, recv)


def solution(mesh):
    devices = mesh.devices.transpose([mesh.axis_names.index("scan"), mesh.axis_names.index("tile")])
    n_scan, n_tile = devices.shape
    n_sx = 4 if n_scan % 4 == 0 else 1
    sub = Mesh(devices.reshape(n_scan // n_sx, n_sx, n_tile), ("sy", "sx", "tile"))
    return jax.shard_map(
        per_device,
        mesh=sub,
        in_specs=(
            P("tile", SCAN_AXES, None),
            P("tile", SCAN_AXES),
            P("tile"),
            P("tile"),
            P("tile", None),
            P(),
        ),
        out_specs=P("tile", SCAN_AXES),
        check_vma=False,
    )
```

```python
import jax
import jax.numpy as jnp
from jax import lax
from jax.experimental import pallas as pl
from jax.experimental.pallas import tpu as pltpu
from jax.sharding import Mesh, PartitionSpec as P

DEG_MAX = 8
NGB = 24
SCAN_AXES = ("sy", "sx")


def build_templates(ground_rows, position, lengths, degrees, block):
    position = position.astype(jnp.float32)
    length_value = lengths.astype(jnp.float32)[:, None]
    inside = position[None, :] < length_value
    coord = 2.0 * (position[None, :] + 0.5) / length_value - 1.0
    column = jnp.arange(block)[None, None, :]
    out = jnp.zeros(ground_rows.shape + (block,), jnp.float32)
    previous = jnp.ones_like(coord)
    current = coord
    for degree in range(1, DEG_MAX + 1):
        keep = jnp.logical_and(inside, (degree <= degrees)[:, None])
        value = jnp.where(keep, current, jnp.float32(0.0))
        out = jnp.where(column == degree - 1, value[:, :, None], out)
        following = ((2.0 * degree + 1.0) * coord * current - degree * previous) / (degree + 1.0)
        previous, current = (current, following)
    hit = jnp.logical_and(ground_rows[:, :, None] + DEG_MAX == column, inside[:, :, None])
    hit = jnp.logical_and(hit, column < DEG_MAX + NGB)
    out = jnp.where(hit, jnp.float32(1.0), out)
    return out.astype(jnp.bfloat16)


def per_device(pointing, ground_bin, degrees, lengths, tile_lists, owner_map):
    scan_count, sample_rows, width = pointing.shape
    n_sy = lax.axis_size("sy")
    n_sx = lax.axis_size("sx")
    n_scan = n_sy * n_sx
    n_tile = lax.axis_size("tile")
    sy = lax.axis_index("sy")
    sx = lax.axis_index("sx")
    scan_index = sy * n_sx + sx
    k_tiles = tile_lists.shape[1]
    tile_pixels = width // k_tiles
    col_width = tile_pixels
    half = k_tiles // 2 + 1
    template_cols = DEG_MAX + NGB

    position = scan_index * sample_rows + jnp.arange(sample_rows)
    inside = position[None, :] < lengths[:, None]
    masked = jnp.where(inside[:, :, None], pointing, jnp.zeros_like(pointing))
    template = build_templates(ground_bin, position, lengths, degrees, tile_pixels)
    local = jnp.concatenate([masked, template], axis=2)

    def shifted(x, axis, n, d):
        return lax.ppermute(x, axis, [(i, (i + d) % n) for i in range(n)])

    def column_sums(one, gather_axis, n_gather, reduce_axis, n_reduce, reduce_index):
        rows_all = jnp.concatenate(
            [one] + [shifted(one, gather_axis, n_gather, d) for d in range(1, n_gather)], axis=1
        )
        rows = rows_all[:, :, :width]
        tpl = rows_all[:, :, width : width + template_cols]
        if reduce_axis == "sy":
            firsts = [((reduce_index + d) % n_reduce) * n_sx + sx for d in range(n_reduce)]
        else:
            firsts = [sy * n_sx + (reduce_index + d) % n_reduce for d in range(n_reduce)]
        cols = jnp.concatenate(
            [lax.dynamic_slice_in_dim(rows, f * tile_pixels, tile_pixels, 2) for f in firsts], axis=2
        )
        grams = jnp.einsum("snp,snq->pq", rows, cols, preferred_element_type=jnp.float32)
        projs = jnp.einsum("snt,snp->tp", tpl, rows, preferred_element_type=jnp.float32)
        projs = jnp.swapaxes(projs.reshape(template_cols, k_tiles, tile_pixels), 0, 1)
        projs = projs.reshape(k_tiles * template_cols, tile_pixels)
        summed = None
        for d in range(n_reduce):
            part = jnp.concatenate([grams[:, d * col_width : (d + 1) * col_width], projs], axis=0)
            part = part if d == 0 else shifted(part, reduce_axis, n_reduce, d)
            summed = part if summed is None else summed + part
        norm = jnp.einsum("snt,snu->tu", tpl, tpl, preferred_element_type=jnp.float32)
        norm = norm + sum(shifted(norm, reduce_axis, n_reduce, d) for d in range(1, n_reduce))
        return summed, norm

    first = column_sums(local[0:1], "sx", n_sx, "sy", n_sy, sy)
    second = column_sums(local[1:2], "sy", n_sy, "sx", n_sx, sx)
    summed = jnp.stack([first[0], second[0]])
    normal = jnp.stack([first[1], second[1]]) + jnp.eye(template_cols, dtype=jnp.float32)[None]
    factor = jnp.linalg.cholesky(normal)
    eye = jnp.broadcast_to(jnp.eye(template_cols, dtype=jnp.float32), normal.shape)
    inverse = jax.scipy.linalg.solve_triangular(factor, eye, lower=True)
    gram = summed[:, :width]
    proj = summed[:, width : width + k_tiles * template_cols].reshape(scan_count, k_tiles, template_cols, tile_pixels)
    proj = jnp.swapaxes(proj, 1, 2).reshape(scan_count, template_cols, width)
    whitened = jnp.einsum("stu,sup->stp", inverse, proj, precision=lax.Precision.HIGH)
    w_col = lax.dynamic_slice_in_dim(whitened, scan_index * tile_pixels, tile_pixels, 2)
    correction = jnp.einsum("stp,stq->spq", whitened, w_col, precision=lax.Precision.HIGH)
    contrib = gram - correction

    k_cols = 1
    tile_rows = contrib.reshape(scan_count * k_tiles, tile_pixels, col_width)
    row_tiles = tile_lists.reshape(-1)
    matches = row_tiles[:, None] == jnp.arange(owner_map.shape[0])[None, :]
    owners = jnp.sum(jnp.where(matches, owner_map[None, :], 0), axis=1)
    row_total = scan_count * k_tiles
    capacity = row_total // n_tile
    ordering = jnp.argsort(owners * row_total + jnp.arange(row_total), stable=True)
    local_cols = (
        lax.dynamic_slice_in_dim(tile_lists, scan_index * k_cols, k_cols, 1) - scan_index * n_tile
    )
    local_cols = jnp.repeat(local_cols, k_tiles, axis=0)
    labels = jnp.concatenate([(row_tiles // n_tile)[:, None], local_cols], axis=1)
    send_rows = tile_rows[ordering].reshape(n_tile, capacity, tile_pixels, col_width)
    send_labels = labels[ordering].reshape(n_tile, capacity, 1 + k_cols)
    recv_rows, recv_labels = (
        lax.all_to_all(send_rows, "tile", split_axis=0, concat_axis=0, tiled=True),
        lax.all_to_all(send_labels, "tile", split_axis=0, concat_axis=0, tiled=True),
    )
    item_total = n_tile * capacity
    recv_rows = recv_rows.reshape(item_total, tile_pixels, tile_pixels)
    recv_labels = recv_labels.reshape(item_total, 1 + k_cols)
    row_block = recv_labels[:, 0]
    order = jnp.argsort(row_block).astype(jnp.int32)
    counts = jnp.sum(row_block[:, None] == jnp.arange(n_scan)[None, :], axis=0)
    starts = jnp.concatenate([jnp.zeros((1,), jnp.int32), jnp.cumsum(counts).astype(jnp.int32)])
    return place(recv_rows, order, starts, recv_labels[:, 1], n_scan, n_tile)


def place(recv, order, starts, col_block, n_rows, n_cols):
    items, tile_pixels, _ = recv.shape

    group = 8 if n_rows % 8 == 0 else 1

    def kernel(order_ref, starts_ref, col_ref, recv_ref, out_ref):
        r = pl.program_id(0)
        out_ref[...] = jnp.zeros(out_ref.shape, out_ref.dtype)
        for q in range(group):

            def body(k, carry, q=q):
                i = order_ref[k]
                at = pl.ds(pl.multiple_of(col_ref[i] * tile_pixels, tile_pixels), tile_pixels)
                out_ref[q * tile_pixels : (q + 1) * tile_pixels, at] += recv_ref[i]
                return carry

            lax.fori_loop(starts_ref[r * group + q], starts_ref[r * group + q + 1], body, 0)

    return pl.pallas_call(
        kernel,
        grid_spec=pltpu.PrefetchScalarGridSpec(
            num_scalar_prefetch=3,
            grid=(n_rows // group,),
            in_specs=[pl.BlockSpec((items, tile_pixels, tile_pixels), lambda r, a, b, c: (0, 0, 0))],
            out_specs=pl.BlockSpec((group * tile_pixels, n_cols * tile_pixels), lambda r, a, b, c: (r, 0)),
        ),
        out_shape=jax.ShapeDtypeStruct((n_rows * tile_pixels, n_cols * tile_pixels), jnp.float32),
    )(order, starts, col_block, recv)


def solution(mesh):
    devices = mesh.devices.transpose([mesh.axis_names.index("scan"), mesh.axis_names.index("tile")])
    n_scan, n_tile = devices.shape
    n_sx = 4 if n_scan % 4 == 0 else 1
    sub = Mesh(devices.reshape(n_scan // n_sx, n_sx, n_tile), ("sy", "sx", "tile"))
    return jax.shard_map(
        per_device,
        mesh=sub,
        in_specs=(
            P("tile", SCAN_AXES, None),
            P("tile", SCAN_AXES),
            P("tile"),
            P("tile"),
            P("tile", None),
            P(),
        ),
        out_specs=P("tile", SCAN_AXES),
        check_vma=False,
    )
```

```python
import jax
import jax.numpy as jnp
from jax import lax
from jax.experimental import pallas as pl
from jax.experimental.pallas import tpu as pltpu
from jax.sharding import Mesh, PartitionSpec as P

DEG_MAX = 8
NGB = 24
SCAN_AXES = ("sy", "sx")


def build_templates(ground_rows, position, lengths, degrees, block):
    position = position.astype(jnp.float32)
    length_value = lengths.astype(jnp.float32)[:, None]
    inside = position[None, :] < length_value
    coord = 2.0 * (position[None, :] + 0.5) / length_value - 1.0
    column = jnp.arange(block)[None, None, :]
    out = jnp.zeros(ground_rows.shape + (block,), jnp.float32)
    previous = jnp.ones_like(coord)
    current = coord
    for degree in range(1, DEG_MAX + 1):
        keep = jnp.logical_and(inside, (degree <= degrees)[:, None])
        value = jnp.where(keep, current, jnp.float32(0.0))
        out = jnp.where(column == degree - 1, value[:, :, None], out)
        following = ((2.0 * degree + 1.0) * coord * current - degree * previous) / (degree + 1.0)
        previous, current = (current, following)
    hit = jnp.logical_and(ground_rows[:, :, None] + DEG_MAX == column, inside[:, :, None])
    hit = jnp.logical_and(hit, column < DEG_MAX + NGB)
    out = jnp.where(hit, jnp.float32(1.0), out)
    return out.astype(jnp.bfloat16)


def per_device(pointing, ground_bin, degrees, lengths, tile_lists, owner_map):
    scan_count, sample_rows, width = pointing.shape
    n_sy = lax.axis_size("sy")
    n_sx = lax.axis_size("sx")
    n_scan = n_sy * n_sx
    n_tile = lax.axis_size("tile")
    sy = lax.axis_index("sy")
    sx = lax.axis_index("sx")
    scan_index = sy * n_sx + sx
    k_tiles = tile_lists.shape[1]
    tile_pixels = width // k_tiles
    col_width = tile_pixels
    half = k_tiles // 2 + 1
    template_cols = DEG_MAX + NGB

    position = scan_index * sample_rows + jnp.arange(sample_rows)
    inside = position[None, :] < lengths[:, None]
    masked = jnp.where(inside[:, :, None], pointing, jnp.zeros_like(pointing))
    template = build_templates(ground_bin, position, lengths, degrees, tile_pixels)
    local = jnp.concatenate([masked, template], axis=2)

    def shifted(x, axis, n, d):
        return lax.ppermute(x, axis, [(i, (i + d) % n) for i in range(n)])

    def column_sums(one, gather_axis, n_gather, reduce_axis, n_reduce, reduce_index):
        rows_all = jnp.concatenate(
            [one] + [shifted(one, gather_axis, n_gather, d) for d in range(1, n_gather)], axis=1
        )
        rows = rows_all[:, :, :width]
        tpl = rows_all[:, :, width : width + template_cols]
        if reduce_axis == "sy":
            firsts = [((reduce_index + d) % n_reduce) * n_sx + sx for d in range(n_reduce)]
        else:
            firsts = [sy * n_sx + (reduce_index + d) % n_reduce for d in range(n_reduce)]
        cols = jnp.concatenate(
            [lax.dynamic_slice_in_dim(rows, f * tile_pixels, tile_pixels, 2) for f in firsts], axis=2
        )
        grams = jnp.einsum("snp,snq->pq", rows, cols, preferred_element_type=jnp.float32)
        projs = jnp.einsum("snt,snp->tp", tpl, rows, preferred_element_type=jnp.float32)
        projs = jnp.swapaxes(projs.reshape(template_cols, k_tiles, tile_pixels), 0, 1)
        projs = projs.reshape(k_tiles * template_cols, tile_pixels)
        summed = None
        for d in range(n_reduce):
            part = jnp.concatenate([grams[:, d * col_width : (d + 1) * col_width], projs], axis=0)
            part = part if d == 0 else shifted(part, reduce_axis, n_reduce, d)
            summed = part if summed is None else summed + part
        norm = jnp.einsum("snt,snu->tu", tpl, tpl, preferred_element_type=jnp.float32)
        norm = norm + sum(shifted(norm, reduce_axis, n_reduce, d) for d in range(1, n_reduce))
        return summed, norm

    first = column_sums(local[0:1], "sx", n_sx, "sy", n_sy, sy)
    second = column_sums(local[1:2], "sy", n_sy, "sx", n_sx, sx)
    summed = jnp.stack([first[0], second[0]])
    normal = jnp.stack([first[1], second[1]]) + jnp.eye(template_cols, dtype=jnp.float32)[None]
    factor = jnp.linalg.cholesky(normal)
    eye = jnp.broadcast_to(jnp.eye(template_cols, dtype=jnp.float32), normal.shape)
    inverse = jax.scipy.linalg.solve_triangular(factor, eye, lower=True)
    gram = summed[:, :width]
    proj = summed[:, width : width + k_tiles * template_cols].reshape(scan_count, k_tiles, template_cols, tile_pixels)
    proj = jnp.swapaxes(proj, 1, 2).reshape(scan_count, template_cols, width)
    whitened = jnp.einsum("stu,sup->stp", inverse, proj, precision=lax.Precision.HIGH)
    w_col = lax.dynamic_slice_in_dim(whitened, scan_index * tile_pixels, tile_pixels, 2)
    correction = jnp.einsum("stp,stq->spq", whitened, w_col, precision=lax.Precision.HIGH)
    contrib = gram - correction

    k_cols = 1
    tile_rows = contrib.reshape(scan_count * k_tiles, tile_pixels, col_width)
    row_tiles = tile_lists.reshape(-1)
    matches = row_tiles[:, None] == jnp.arange(owner_map.shape[0])[None, :]
    owners = jnp.sum(jnp.where(matches, owner_map[None, :], 0), axis=1)
    row_total = scan_count * k_tiles
    capacity = row_total // n_tile
    ordering = jnp.argsort(owners * row_total + jnp.arange(row_total), stable=True)
    local_cols = (
        lax.dynamic_slice_in_dim(tile_lists, scan_index * k_cols, k_cols, 1) - scan_index * n_tile
    )
    local_cols = jnp.repeat(local_cols, k_tiles, axis=0)
    labels = jnp.concatenate([(row_tiles // n_tile)[:, None], local_cols], axis=1)
    send_rows = tile_rows[ordering].reshape(n_tile, capacity, tile_pixels, col_width)
    send_labels = labels[ordering].reshape(n_tile, capacity, 1 + k_cols)
    recv_rows, recv_labels = (
        lax.all_to_all(send_rows, "tile", split_axis=0, concat_axis=0, tiled=True),
        lax.all_to_all(send_labels, "tile", split_axis=0, concat_axis=0, tiled=True),
    )
    item_total = n_tile * capacity
    recv_rows = recv_rows.reshape(item_total, tile_pixels, tile_pixels)
    recv_labels = recv_labels.reshape(item_total, 1 + k_cols)
    row_block = recv_labels[:, 0]
    order = jnp.argsort(row_block).astype(jnp.int32)
    counts = jnp.sum(row_block[:, None] == jnp.arange(n_scan)[None, :], axis=0)
    starts = jnp.concatenate([jnp.zeros((1,), jnp.int32), jnp.cumsum(counts).astype(jnp.int32)])
    return place(recv_rows, order, starts, recv_labels[:, 1], n_scan, n_tile)


def place(recv, order, starts, col_block, n_rows, n_cols):
    items, tile_pixels, _ = recv.shape

    group = 2 if n_rows % 2 == 0 else 1

    def kernel(order_ref, starts_ref, col_ref, recv_ref, out_ref):
        r = pl.program_id(0)
        out_ref[...] = jnp.zeros(out_ref.shape, out_ref.dtype)
        for q in range(group):

            def body(k, carry, q=q):
                i = order_ref[k]
                at = pl.ds(pl.multiple_of(col_ref[i] * tile_pixels, tile_pixels), tile_pixels)
                out_ref[q * tile_pixels : (q + 1) * tile_pixels, at] += recv_ref[i]
                return carry

            lax.fori_loop(starts_ref[r * group + q], starts_ref[r * group + q + 1], body, 0)

    return pl.pallas_call(
        kernel,
        grid_spec=pltpu.PrefetchScalarGridSpec(
            num_scalar_prefetch=3,
            grid=(n_rows // group,),
            in_specs=[pl.BlockSpec((items, tile_pixels, tile_pixels), lambda r, a, b, c: (0, 0, 0))],
            out_specs=pl.BlockSpec((group * tile_pixels, n_cols * tile_pixels), lambda r, a, b, c: (r, 0)),
        ),
        out_shape=jax.ShapeDtypeStruct((n_rows * tile_pixels, n_cols * tile_pixels), jnp.float32),
    )(order, starts, col_block, recv)


def solution(mesh):
    devices = mesh.devices.transpose([mesh.axis_names.index("scan"), mesh.axis_names.index("tile")])
    n_scan, n_tile = devices.shape
    n_sx = 4 if n_scan % 4 == 0 else 1
    sub = Mesh(devices.reshape(n_scan // n_sx, n_sx, n_tile), ("sy", "sx", "tile"))
    return jax.shard_map(
        per_device,
        mesh=sub,
        in_specs=(
            P("tile", SCAN_AXES, None),
            P("tile", SCAN_AXES),
            P("tile"),
            P("tile"),
            P("tile", None),
            P(),
        ),
        out_specs=P("tile", SCAN_AXES),
        check_vma=False,
    )
```
